512 devices in a mesh: section: 4 (over y), ctx: 16 (over z), dp: 8 (over x, core).
Axes of the slice: x: 4, y: 4, z: 16, core: 2. Of those that a mesh axis runs over, the one named last changes fastest.
Arguments:
- query_input: bfloat16 [4, 8, 2048, 4096], P('section', 'dp', 'ctx'), may hold values from -6 to 6
- key_states: bfloat16 [4, 8, 2048, 512], P('section', 'dp', 'ctx'), may hold values from -4 to 4
- value_states: bfloat16 [4, 8, 2048, 512], P('section', 'dp', 'ctx'), may hold values from -16 to 16
- query_gain: float32 [4, 4096], P('section', 'ctx'), may hold values from 0.5 to 1.5
- top_grad: bfloat16 [8, 2048, 4096], P('dp', 'ctx'), may hold values from -6 to 6
- block_lists: int32 [16, 4], replicated, may hold values from 0 to 15, as said below
Outputs:
- stream_grad: bfloat16 [4, 8, 2048, 4096], P('section', 'dp', 'ctx')
- key_grad: bfloat16 [4, 8, 2048, 512], P('section', 'dp', 'ctx')
- value_grad: bfloat16 [4, 8, 2048, 512], P('section', 'dp', 'ctx')
- gain_grad: float32 [4, 4096], P('section', 'ctx')
The draws below stay inside these ranges and needn't reach their ends.
Inputs may be any that keep to these rules, and one draw needn't show every extreme that they name: `block_lists`: row b names 4 different blocks; the window blocks b - 1, b, b + 1 that exist come first, then block 0, then block 15, then blocks drawn at random, as far as 4 allows.
All inputs are finite; a program needn't handle non-finite values.
Results may differ from the reference program's by a relative error of at most 0.03.
Values may be sent and summed in bfloat16 or wider, within the bound.
No kernel may reach another device: no remote copies, remote signals or barrier semaphores. Data moves between devices by JAX's collectives and lax.ppermute only.
A program may use at most 64 MiB of HBM per device.

```python
import jax
import jax.numpy as jnp
from jax import lax

HEAD_FEATURES = 128
QUERY_HEADS = 32
KEY_VALUE_HEADS = 4
BLOCK_POSITIONS = 128
SECTION_LAYERS = 4
REPLICA_COUNT = 8
SEQUENCE_TOKENS = 2048
HD = 4096
KVD = 512
SEQUENCE_BLOCKS = 16
LISTED_BLOCKS = 4


def drawn_keys(key):
    base = jax.random.fold_in(key, 7)
    array_shape = (SECTION_LAYERS, REPLICA_COUNT, SEQUENCE_TOKENS, KVD)
    states = jnp.clip(jax.random.normal(jax.random.fold_in(base, 1), array_shape, jnp.float32), -4.0, 4.0)
    return states


def draw_key_states(key, part):
    states = drawn_keys(key)
    return states.astype(jnp.bfloat16)


def draw_query_input(key, part):
    array_shape = (SECTION_LAYERS, REPLICA_COUNT, SEQUENCE_TOKENS, HD)
    noise_key = jax.random.fold_in(key, 19)
    return jnp.clip(jax.random.normal(noise_key, array_shape, jnp.float32), -6.0, 6.0).astype(jnp.bfloat16)


def draw_block_lists(key, part):
    rows_at = jnp.arange(SEQUENCE_BLOCKS, dtype=jnp.int32)[:, None]
    cols_at = jnp.arange(SEQUENCE_BLOCKS, dtype=jnp.int32)[None, :]
    nearby = jnp.abs(rows_at - cols_at) <= 1
    first_col = cols_at == 0
    last_col = cols_at == SEQUENCE_BLOCKS - 1
    ranks = jnp.where(nearby, 4, jnp.where(first_col, 3, jnp.where(last_col, 2, 1))).astype(jnp.int32)
    jitter = jax.random.randint(jax.random.fold_in(key, 23), (SEQUENCE_BLOCKS, SEQUENCE_BLOCKS), 0, 4 * SEQUENCE_BLOCKS).astype(jnp.int32)
    scores = ranks * (8 * SEQUENCE_BLOCKS * SEQUENCE_BLOCKS) + jitter * SEQUENCE_BLOCKS + cols_at
    picked = lax.top_k(scores, LISTED_BLOCKS)[1]
    return picked.astype(jnp.int32)


def level_of(rng, shape, pieces, smallest, top_value):
    gain, own = 1.0, jax.random.fold_in(rng, 6)
    for dim, shards_of in pieces:
        steps = jnp.exp(jax.random.uniform(jax.random.fold_in(own, dim), (shards_of,), jnp.float32, smallest / len(pieces), top_value / len(pieces)))
        gain = gain * jnp.repeat(steps, shape[dim] // shards_of).reshape([-1 if axis == dim else 1 for axis in range(len(shape))])
    return gain


def noise(rng, dims, width, most, split=(), kind=jnp.bfloat16):
    values = jax.random.normal(rng, dims, jnp.float32) * width
    if len(split) > 0:
        values = level_of(rng, dims, split, -0.22, 0.18) * values
    return jnp.clip(values, min=-most, max=most).astype(kind)


def setup_inputs(seed: int = 0) -> dict:
    splits = jax.random.split(jax.random.key(seed), 7)
    query_input = draw_query_input(jax.random.fold_in(splits[6], 71), 0)
    key_states = draw_key_states(jax.random.fold_in(splits[6], 71), 0)
    value_states = noise(splits[2], (SECTION_LAYERS, REPLICA_COUNT, SEQUENCE_TOKENS, KVD), 4.0, 16.0, ((0, 4), (1, 8), (2, 16)))
    query_gain = jnp.clip(1.0 + 0.1 * jax.random.normal(splits[3], (SECTION_LAYERS, HD), jnp.float32), 0.5, 1.5)
    top_grad = noise(splits[4], (REPLICA_COUNT, SEQUENCE_TOKENS, HD), 1.0, 6.0, ((0, 8), (1, 16)))
    block_lists = draw_block_lists(jax.random.fold_in(splits[6], 71), 0)
    return {"query_input": query_input, "key_states": key_states, "value_states": value_states, "query_gain": query_gain, "top_grad": top_grad, "block_lists": block_lists}


def layer_grads(layer_input, rowwise_keys, rowwise_values, gain_row, gradient_rows, block_lists):
    group_width = QUERY_HEADS // KEY_VALUE_HEADS
    scale_factor = 1.0 / (HEAD_FEATURES ** 0.5)
    query_rows = (layer_input.astype(jnp.float32) * gain_row).astype(jnp.bfloat16)
    blocked_queries = query_rows.reshape(SEQUENCE_BLOCKS, BLOCK_POSITIONS, KEY_VALUE_HEADS, group_width, HEAD_FEATURES)
    gradient_blocks = gradient_rows.reshape(SEQUENCE_BLOCKS, BLOCK_POSITIONS, KEY_VALUE_HEADS, group_width, HEAD_FEATURES)
    blocked_keys = rowwise_keys.reshape(SEQUENCE_BLOCKS, BLOCK_POSITIONS, KEY_VALUE_HEADS, HEAD_FEATURES)
    blocked_values = rowwise_values.reshape(SEQUENCE_BLOCKS, BLOCK_POSITIONS, KEY_VALUE_HEADS, HEAD_FEATURES)

    def one_block(inputs_now):
        query_here, grad_here, current_list = inputs_now
        neighbor_keys = blocked_keys[current_list].reshape(LISTED_BLOCKS * BLOCK_POSITIONS, KEY_VALUE_HEADS, HEAD_FEATURES).astype(jnp.float32)
        neighbor_values = blocked_values[current_list].reshape(LISTED_BLOCKS * BLOCK_POSITIONS, KEY_VALUE_HEADS, HEAD_FEATURES).astype(jnp.float32)
        query_wide = query_here.astype(jnp.float32)
        grad_wide = grad_here.astype(jnp.float32)
        scores = jnp.einsum("bkgd,jkd->kgbj", query_wide, neighbor_keys) * scale_factor
        row_max = jnp.max(scores, axis=-1, keepdims=True)
        weights = jnp.exp(scores - row_max)
        probs = weights / jnp.sum(weights, axis=-1, keepdims=True)
        probs_low = lax.optimization_barrier(probs.astype(jnp.bfloat16)).astype(jnp.float32)
        prob_grad = jnp.einsum("bkgd,jkd->kgbj", grad_wide, neighbor_values)
        row_dot = jnp.sum(probs * prob_grad, axis=-1, keepdims=True)
        score_grad = lax.optimization_barrier((probs * (prob_grad - row_dot)).astype(jnp.bfloat16)).astype(jnp.float32)
        query_grad = jnp.einsum("kgbj,jkd->bkgd", score_grad, neighbor_keys) * scale_factor
        key_part = jnp.einsum("kgbj,bkgd->jkd", score_grad, query_wide) * scale_factor
        value_part = jnp.einsum("kgbj,bkgd->jkd", probs_low, grad_wide)
        return query_grad, key_part, value_part

    query_grad, key_pieces, value_pieces = lax.map(one_block, (blocked_queries, gradient_blocks, block_lists))
    target_labels = block_lists.reshape(-1)
    key_gradient_sum = jnp.zeros((SEQUENCE_BLOCKS, BLOCK_POSITIONS, KEY_VALUE_HEADS, HEAD_FEATURES), jnp.float32).at[target_labels].add(key_pieces.reshape(SEQUENCE_BLOCKS * LISTED_BLOCKS, BLOCK_POSITIONS, KEY_VALUE_HEADS, HEAD_FEATURES))
    value_gradient_sum = jnp.zeros((SEQUENCE_BLOCKS, BLOCK_POSITIONS, KEY_VALUE_HEADS, HEAD_FEATURES), jnp.float32).at[target_labels].add(value_pieces.reshape(SEQUENCE_BLOCKS * LISTED_BLOCKS, BLOCK_POSITIONS, KEY_VALUE_HEADS, HEAD_FEATURES))
    query_grad = query_grad.reshape(SEQUENCE_TOKENS, HD)
    moved_grad = (gain_row * query_grad).astype(jnp.bfloat16)
    stream_rows = (gradient_rows.astype(jnp.float32) + moved_grad.astype(jnp.float32)).astype(jnp.bfloat16)
    gain_part = jnp.sum(layer_input.astype(jnp.float32) * query_grad, axis=0)
    key_out = key_gradient_sum.reshape(SEQUENCE_TOKENS, KVD).astype(jnp.bfloat16)
    value_out = value_gradient_sum.reshape(SEQUENCE_TOKENS, KVD).astype(jnp.bfloat16)
    return stream_rows, key_out, value_out, gain_part


def reference(query_input, key_states, value_states, query_gain, top_grad, block_lists):
    stream_out = [[None] * REPLICA_COUNT for section_at in range(SECTION_LAYERS)]
    key_out = [[None] * REPLICA_COUNT for section_at in range(SECTION_LAYERS)]
    value_out = [[None] * REPLICA_COUNT for section_at in range(SECTION_LAYERS)]
    gain_out = [jnp.zeros((HD,), jnp.float32) for section_at in range(SECTION_LAYERS)]
    for replica in range(REPLICA_COUNT):
        incoming = top_grad[replica]
        for section_at in reversed(range(SECTION_LAYERS)):
            stream_rows, rowwise_keys, rowwise_values, gain_part = layer_grads(
                query_input[section_at, replica], key_states[section_at, replica], value_states[section_at, replica],
                query_gain[section_at], incoming, block_lists)
            stream_out[section_at][replica] = stream_rows
            key_out[section_at][replica] = rowwise_keys
            value_out[section_at][replica] = rowwise_values
            gain_out[section_at] = gain_out[section_at] + gain_part
            incoming = stream_rows
    stream_all = jnp.stack([jnp.stack(row_list) for row_list in stream_out])
    key_all = jnp.stack([jnp.stack(row_list) for row_list in key_out])
    value_all = jnp.stack([jnp.stack(row_list) for row_list in value_out])
    return stream_all, key_all, value_all, jnp.stack(gain_out)
```

```python
import math

import jax
import jax.numpy as jnp
from jax import lax
from jax.sharding import PartitionSpec as P

HEAD_FEATURES = 128


def passed_along(block, axis, distance):
    devices = range(lax.axis_size(axis))
    route = [(i - distance, i) for i in devices if i - distance in devices]
    return lax.ppermute(block, axis, route)


def shards(query_input, key_states, value_states, query_gain, top_grad, block_lists):
    ctx_count = lax.axis_size("ctx")
    section_count = lax.axis_size("section")
    section_pos = lax.axis_index("section")
    ctx_pos = lax.axis_index("ctx")
    layer_input = query_input[0, 0]
    tok_local, feature_count = layer_input.shape
    kv_width = key_states.shape[-1]
    kv_heads = kv_width // HEAD_FEATURES
    head_count = feature_count // HEAD_FEATURES
    group_width = head_count // kv_heads
    group_features = group_width * HEAD_FEATURES
    block_count, listed = block_lists.shape
    block_rows = tok_local * ctx_count // block_count
    assert block_rows == tok_local
    scale_factor = 1.0 / math.sqrt(HEAD_FEATURES)
    turn_count = kv_heads + section_count - 1

    gain_row = lax.all_gather(query_gain[0], "ctx", tiled=True)
    query_rows = (layer_input.astype(jnp.float32) * gain_row).astype(jnp.bfloat16)
    own_top = top_grad[0]
    own_keys = key_states[0, 0]
    own_values = value_states[0, 0]
    own_list = lax.dynamic_index_in_dim(block_lists, ctx_pos, 0, keepdims=False)
    on_top = section_pos == section_count - 1
    lag = section_count - 1 - section_pos

    def group_cols(array, group, width):
        return lax.dynamic_slice_in_dim(array, group * width, width, 1)

    def attend(group, head_grad):
        keys_now = lax.all_gather(group_cols(own_keys, group, HEAD_FEATURES), "ctx", tiled=True)
        values_now = lax.all_gather(group_cols(own_values, group, HEAD_FEATURES), "ctx", tiled=True)
        neighbor_keys = keys_now.reshape(block_count, block_rows, HEAD_FEATURES)[own_list].reshape(
            listed * block_rows, HEAD_FEATURES
        )
        neighbor_values = values_now.reshape(block_count, block_rows, HEAD_FEATURES)[
            own_list
        ].reshape(listed * block_rows, HEAD_FEATURES)
        query_now = group_cols(query_rows, group, group_features).reshape(
            tok_local, group_width, HEAD_FEATURES
        )
        input_now = group_cols(layer_input, group, group_features)
        gain_now = lax.dynamic_slice_in_dim(gain_row, group * group_features, group_features, 0)
        grad_now = head_grad.reshape(tok_local, group_width, HEAD_FEATURES)
        scores = (
            jnp.einsum("bhd,jd->hbj", query_now, neighbor_keys, preferred_element_type=jnp.float32)
            * scale_factor
        )
        row_max = jnp.max(scores, axis=-1, keepdims=True)
        weights = jnp.exp(scores - row_max)
        probs = weights / jnp.sum(weights, axis=-1, keepdims=True)
        probs_low = probs.astype(jnp.bfloat16)
        prob_grad = jnp.einsum(
            "bhd,jd->hbj", grad_now, neighbor_values, preferred_element_type=jnp.float32
        )
        row_dot = jnp.sum(probs * prob_grad, axis=-1, keepdims=True)
        score_grad = (probs * (prob_grad - row_dot)).astype(jnp.bfloat16)
        query_grad = (
            jnp.einsum("hbj,jd->bhd", score_grad, neighbor_keys, preferred_element_type=jnp.float32)
            * scale_factor
        ).reshape(tok_local, group_features)
        key_part = (
            jnp.einsum("hbj,bhd->jd", score_grad, query_now, preferred_element_type=jnp.float32)
            * scale_factor
        )
        value_part = jnp.einsum(
            "hbj,bhd->jd", probs_low, grad_now, preferred_element_type=jnp.float32
        )
        moved_grad = (gain_now * query_grad).astype(jnp.bfloat16)
        handed = (head_grad.astype(jnp.float32) + moved_grad.astype(jnp.float32)).astype(
            jnp.bfloat16
        )
        gain_part = jnp.sum(input_now.astype(jnp.float32) * query_grad, axis=0)
        key_blocks = (
            jnp.zeros((block_count, block_rows, HEAD_FEATURES), jnp.float32)
            .at[own_list]
            .add(key_part.reshape(listed, block_rows, HEAD_FEATURES))
        )
        value_blocks = (
            jnp.zeros((block_count, block_rows, HEAD_FEATURES), jnp.float32)
            .at[own_list]
            .add(value_part.reshape(listed, block_rows, HEAD_FEATURES))
        )
        key_own = lax.psum_scatter(
            key_blocks.reshape(block_count * block_rows, HEAD_FEATURES),
            "ctx",
            scatter_dimension=0,
            tiled=True,
        )
        value_own = lax.psum_scatter(
            value_blocks.reshape(block_count * block_rows, HEAD_FEATURES),
            "ctx",
            scatter_dimension=0,
            tiled=True,
        )
        return handed, key_own, value_own, gain_part

    incoming = jnp.zeros((tok_local, group_features), jnp.bfloat16)
    handed_turns, key_turns, value_turns, gain_turns = [], [], [], []
    for turn in range(turn_count):
        group = jnp.clip(turn - lag, 0, kv_heads - 1)
        from_top = group_cols(own_top, group, group_features)
        head_grad = jnp.where(on_top, from_top, incoming)
        handed, key_own, value_own, gain_part = attend(group, head_grad)
        handed_turns.append(handed)
        key_turns.append(key_own)
        value_turns.append(value_own)
        gain_turns.append(gain_part)
        if turn + 1 < turn_count:
            incoming = passed_along(handed, "section", -1)

    def own_turns(parts):
        stacked = jnp.stack(parts)
        return lax.dynamic_slice_in_dim(stacked, lag, kv_heads, 0)

    stream_out = (
        own_turns(handed_turns).transpose(1, 0, 2).reshape(tok_local, feature_count)
    )
    key_out = (
        own_turns(key_turns).transpose(1, 0, 2).reshape(tok_local, kv_width).astype(jnp.bfloat16)
    )
    value_out = (
        own_turns(value_turns)
        .transpose(1, 0, 2)
        .reshape(tok_local, kv_width)
        .astype(jnp.bfloat16)
    )
    gain_full = own_turns(gain_turns).reshape(feature_count)
    gain_total = lax.psum(
        lax.psum_scatter(gain_full, "ctx", scatter_dimension=0, tiled=True), "dp"
    )
    return (stream_out[None, None], key_out[None, None], value_out[None, None], gain_total[None])


def solution(mesh):
    placed = (
        P("section", "dp", "ctx", None),
        P("section", "dp", "ctx", None),
        P("section", "dp", "ctx", None),
        P("section", "ctx"),
        P("dp", "ctx", None),
        P(),
    )
    return jax.shard_map(
        shards,
        mesh=mesh,
        in_specs=placed,
        out_specs=(
            P("section", "dp", "ctx", None),
            P("section", "dp", "ctx", None),
            P("section", "dp", "ctx", None),
            P("section", "ctx"),
        ),
        check_vma=False,
    )
```

```python
import math

import jax
import jax.numpy as jnp
from jax import lax
from jax.sharding import PartitionSpec as P

HEAD_FEATURES = 128


def passed_along(block, axis, distance):
    devices = range(lax.axis_size(axis))
    route = [(i - distance, i) for i in devices if i - distance in devices]
    return lax.ppermute(block, axis, route)


def cyclic_shift(block, axis, distance):
    count = lax.axis_size(axis)
    return lax.ppermute(block, axis, [(i, (i + distance) % count) for i in range(count)])


def checked_pairs(pairs):
    pairs = sorted(set(pairs))
    assert len({a for a, _ in pairs}) == len(pairs)
    assert len({b for _, b in pairs}) == len(pairs)
    return pairs


def forward_pairs(count, hop):
    spread = [(m, m + hop) for m in range(0, count, 2 * hop)]
    to_last = [(c - hop, c) for c in range(count - hop, count)]
    to_first = [(c + hop, c) for c in range(hop)]
    return checked_pairs(spread + to_last + to_first)


def reverse_pairs(count, hop):
    gather = [(m + hop, m) for m in range(0, count, 2 * hop)]
    from_last = [(c, c - hop) for c in range(count - hop, count)]
    from_first = [(c, c + hop) for c in range(hop)]
    return checked_pairs(gather + from_last + from_first)


def shards(query_input, key_states, value_states, query_gain, top_grad, block_lists):
    ctx_count = lax.axis_size("ctx")
    section_count = lax.axis_size("section")
    section_pos = lax.axis_index("section")
    ctx_pos = lax.axis_index("ctx")
    layer_input = query_input[0, 0]
    tok_local, feature_count = layer_input.shape
    kv_width = key_states.shape[-1]
    kv_heads = kv_width // HEAD_FEATURES
    head_count = feature_count // HEAD_FEATURES
    group_width = head_count // kv_heads
    group_features = group_width * HEAD_FEATURES
    block_count, listed = block_lists.shape
    block_rows = tok_local
    assert block_count == ctx_count and listed == 4
    hops = []
    hop = ctx_count // 2
    while hop >= 1:
        hops.append(hop)
        hop //= 2
    assert 2 * hops[0] == ctx_count
    scale_factor = 1.0 / math.sqrt(HEAD_FEATURES)
    turn_count = kv_heads + section_count - 1
    last = ctx_count - 1

    first_row = block_lists[0]
    first_extra = jnp.sum(
        jnp.where((first_row != last) & (first_row != 0) & (first_row != 1), first_row, 0)
    )
    last_row = block_lists[last]
    last_extra = jnp.sum(
        jnp.where((last_row != last - 1) & (last_row != last) & (last_row != 0), last_row, 0)
    )
    to_first_shift = first_extra
    to_last_shift = (last - last_extra) % ctx_count

    def bit_of(value, hop):
        return (value // hop) % 2 == 1

    is_first = ctx_pos == 0
    is_last = ctx_pos == last
    is_second = ctx_pos == 1
    uses_spread = ~(is_first | is_last | is_second)

    gain_row = lax.all_gather(query_gain[0], "ctx", tiled=True)
    query_rows = (layer_input.astype(jnp.float32) * gain_row).astype(jnp.bfloat16)
    own_top = top_grad[0]
    own_kv = jnp.stack([key_states[0, 0], value_states[0, 0]])
    on_top = section_pos == section_count - 1
    lag = section_count - 1 - section_pos

    def group_cols(array, group, width):
        return lax.dynamic_slice_in_dim(array, group * width, width, array.ndim - 1)

    def fetch_pool(group):
        own = group_cols(own_kv, group, HEAD_FEATURES)
        prev_blk = cyclic_shift(own, "ctx", 1)
        next_blk = cyclic_shift(own, "ctx", -1)
        second_blk = lax.ppermute(own, "ctx", [(last, 1)])
        lanes = jnp.stack([own, own, own])
        for hop in hops:
            got = lax.ppermute(lanes, "ctx", forward_pairs(ctx_count, hop))
            spread_lane = jnp.where(ctx_pos % (2 * hop) == hop, got[0], lanes[0])
            first_lane = jnp.where(
                (ctx_pos < hop) & bit_of(to_first_shift, hop), got[1], lanes[1]
            )
            last_lane = jnp.where(
                (ctx_pos >= ctx_count - hop) & bit_of(to_last_shift, hop), got[2], lanes[2]
            )
            lanes = jnp.stack([spread_lane, first_lane, last_lane])
        extra = jnp.where(
            is_first, lanes[1], jnp.where(is_last, lanes[2], jnp.where(is_second, second_blk, lanes[0]))
        )
        return jnp.stack([prev_blk, own, next_blk, extra], axis=1)

    def return_parts(parts):
        prev_part, own_part, next_part, extra_part = parts[:, 0], parts[:, 1], parts[:, 2], parts[:, 3]
        total = own_part + cyclic_shift(prev_part, "ctx", -1) + cyclic_shift(next_part, "ctx", 1)
        total = total + lax.ppermute(extra_part, "ctx", [(1, last)])
        zero = jnp.zeros_like(extra_part)
        lanes = jnp.stack(
            [
                jnp.where(uses_spread, extra_part, zero),
                jnp.where(is_first, extra_part, zero),
                jnp.where(is_last, extra_part, zero),
            ]
        )
        for hop in reversed(hops):
            got = lax.ppermute(lanes, "ctx", reverse_pairs(ctx_count, hop))
            spread_lane = jnp.where(ctx_pos % (2 * hop) == 0, lanes[0] + got[0], lanes[0])
            first_lane = jnp.where(
                bit_of(to_first_shift, hop),
                jnp.where((ctx_pos >= hop) & (ctx_pos < 2 * hop), got[1], zero),
                lanes[1],
            )
            last_lane = jnp.where(
                bit_of(to_last_shift, hop),
                jnp.where(
                    (ctx_pos >= ctx_count - 2 * hop) & (ctx_pos < ctx_count - hop), got[2], zero
                ),
                lanes[2],
            )
            lanes = jnp.stack([spread_lane, first_lane, last_lane])
        return total + jnp.where(is_first, lanes[0], zero) + lanes[1] + lanes[2]

    def attend(group, head_grad):
        pool = fetch_pool(group)
        neighbor_keys = pool[0].reshape(listed * block_rows, HEAD_FEATURES)
        neighbor_values = pool[1].reshape(listed * block_rows, HEAD_FEATURES)
        query_now = group_cols(query_rows, group, group_features).reshape(
            tok_local, group_width, HEAD_FEATURES
        )
        input_now = group_cols(layer_input, group, group_features)
        gain_now = lax.dynamic_slice_in_dim(gain_row, group * group_features, group_features, 0)
        grad_now = head_grad.reshape(tok_local, group_width, HEAD_FEATURES)
        scores = (
            jnp.einsum("bhd,jd->hbj", query_now, neighbor_keys, preferred_element_type=jnp.float32)
            * scale_factor
        )
        row_max = jnp.max(scores, axis=-1, keepdims=True)
        weights = jnp.exp(scores - row_max)
        probs = weights / jnp.sum(weights, axis=-1, keepdims=True)
        probs_low = probs.astype(jnp.bfloat16)
        prob_grad = jnp.einsum(
            "bhd,jd->hbj", grad_now, neighbor_values, preferred_element_type=jnp.float32
        )
        row_dot = jnp.sum(probs * prob_grad, axis=-1, keepdims=True)
        score_grad = (probs * (prob_grad - row_dot)).astype(jnp.bfloat16)
        query_grad = (
            jnp.einsum("hbj,jd->bhd", score_grad, neighbor_keys, preferred_element_type=jnp.float32)
            * scale_factor
        ).reshape(tok_local, group_features)
        key_part = (
            jnp.einsum("hbj,bhd->jd", score_grad, query_now, preferred_element_type=jnp.float32)
            * scale_factor
        )
        value_part = jnp.einsum(
            "hbj,bhd->jd", probs_low, grad_now, preferred_element_type=jnp.float32
        )
        moved_grad = (gain_now * query_grad).astype(jnp.bfloat16)
        handed = (head_grad.astype(jnp.float32) + moved_grad.astype(jnp.float32)).astype(
            jnp.bfloat16
        )
        gain_part = jnp.sum(input_now.astype(jnp.float32) * query_grad, axis=0)
        parts = jnp.stack([key_part, value_part]).reshape(2, listed, block_rows, HEAD_FEATURES)
        return handed, return_parts(parts), gain_part

    incoming = jnp.zeros((tok_local, group_features), jnp.bfloat16)
    handed_turns, kv_turns, gain_turns = [], [], []
    for turn in range(turn_count):
        group = jnp.clip(turn - lag, 0, kv_heads - 1)
        from_top = group_cols(own_top, group, group_features)
        head_grad = jnp.where(on_top, from_top, incoming)
        handed, kv_own, gain_part = attend(group, head_grad)
        handed_turns.append(handed)
        kv_turns.append(kv_own)
        gain_turns.append(gain_part)
        if turn + 1 < turn_count:
            incoming = passed_along(handed, "section", -1)

    def own_turns(parts):
        stacked = jnp.stack(parts)
        return lax.dynamic_slice_in_dim(stacked, lag, kv_heads, 0)

    stream_out = own_turns(handed_turns).transpose(1, 0, 2).reshape(tok_local, feature_count)
    kv_out = own_turns(kv_turns).transpose(1, 2, 0, 3).reshape(2, tok_local, kv_width)
    kv_out = kv_out.astype(jnp.bfloat16)
    gain_full = own_turns(gain_turns).reshape(feature_count)
    gain_total = lax.psum(
        lax.psum_scatter(gain_full, "ctx", scatter_dimension=0, tiled=True), "dp"
    )
    return (stream_out[None, None], kv_out[0][None, None], kv_out[1][None, None], gain_total[None])


def solution(mesh):
    placed = (
        P("section", "dp", "ctx", None),
        P("section", "dp", "ctx", None),
        P("section", "dp", "ctx", None),
        P("section", "ctx"),
        P("dp", "ctx", None),
        P(),
    )
    return jax.shard_map(
        shards,
        mesh=mesh,
        in_specs=placed,
        out_specs=(
            P("section", "dp", "ctx", None),
            P("section", "dp", "ctx", None),
            P("section", "dp", "ctx", None),
            P("section", "ctx"),
        ),
        check_vma=False,
    )
```

```python
import math

import jax
import jax.numpy as jnp
import numpy as np
from jax import lax
from jax.sharding import PartitionSpec as P

HEAD_FEATURES = 128


def passed_along(block, axis, distance):
    devices = range(lax.axis_size(axis))
    route = [(i - distance, i) for i in devices if i - distance in devices]
    return lax.ppermute(block, axis, route)


def shards(query_input, key_states, value_states, query_gain, top_grad, block_lists):
    ctx_count = lax.axis_size("ctx")
    section_count = lax.axis_size("section")
    section_pos = lax.axis_index("section")
    layer_input = query_input[0, 0]
    tok_local, feature_count = layer_input.shape
    kv_width = key_states.shape[-1]
    kv_heads = kv_width // HEAD_FEATURES
    head_count = feature_count // HEAD_FEATURES
    local_heads = head_count // ctx_count
    group_width = head_count // kv_heads
    local_kv = max(1, local_heads // group_width)
    per_kv = local_heads // local_kv
    repeats = ctx_count * local_kv // kv_heads
    local_width = local_heads * HEAD_FEATURES
    slot_width = local_kv * HEAD_FEATURES
    total_rows = tok_local * ctx_count
    block_count, listed = block_lists.shape
    block_rows = total_rows // block_count
    scale_factor = 1.0 / math.sqrt(HEAD_FEATURES)
    slot_index = np.arange(ctx_count * local_kv)
    slot_heads = slot_index // local_kv * local_heads // group_width + slot_index % local_kv
    sent_keys = (
        key_states[0, 0]
        .reshape(tok_local, kv_heads, HEAD_FEATURES)[:, slot_heads]
        .reshape(tok_local, ctx_count * slot_width)
    )
    sent_values = (
        value_states[0, 0]
        .reshape(tok_local, kv_heads, HEAD_FEATURES)[:, slot_heads]
        .reshape(tok_local, ctx_count * slot_width)
    )
    head_input, head_keys, head_values, head_top = (
        lax.all_to_all(layer_input, "ctx", split_axis=1, concat_axis=0, tiled=True),
        lax.all_to_all(sent_keys, "ctx", split_axis=1, concat_axis=0, tiled=True),
        lax.all_to_all(sent_values, "ctx", split_axis=1, concat_axis=0, tiled=True),
        lax.all_to_all(top_grad[0], "ctx", split_axis=1, concat_axis=0, tiled=True),
    )
    gain_row = query_gain[0]
    query_rows = (head_input.astype(jnp.float32) * gain_row).astype(jnp.bfloat16)
    blocked_keys = head_keys.reshape(block_count, block_rows, local_kv, HEAD_FEATURES)
    blocked_values = head_values.reshape(block_count, block_rows, local_kv, HEAD_FEATURES)
    per_turn = 2
    unit_count = block_count // per_turn
    turn_rows = per_turn * block_rows
    token_rows = turn_rows // ctx_count
    turn_count = unit_count + section_count - 1
    grid_shape = (per_turn, block_rows, local_kv, per_kv, HEAD_FEATURES)

    def attend(unit, head_grad):
        first_row = unit * turn_rows
        query_now = lax.dynamic_slice_in_dim(query_rows, first_row, turn_rows, 0).reshape(
            grid_shape
        )
        input_now = lax.dynamic_slice_in_dim(head_input, first_row, turn_rows, 0)
        grad_now = head_grad.reshape(grid_shape)
        lists_now = lax.dynamic_slice_in_dim(block_lists, unit * per_turn, per_turn, 0)
        neighbor_keys = blocked_keys[lists_now].reshape(
            per_turn, listed * block_rows, local_kv, HEAD_FEATURES
        )
        neighbor_values = blocked_values[lists_now].reshape(
            per_turn, listed * block_rows, local_kv, HEAD_FEATURES
        )
        scores = (
            jnp.einsum(
                "pbkgd,pjkd->pkgbj", query_now, neighbor_keys, preferred_element_type=jnp.float32
            )
            * scale_factor
        )
        row_max = jnp.max(scores, axis=-1, keepdims=True)
        weights = jnp.exp(scores - row_max)
        probs = weights / jnp.sum(weights, axis=-1, keepdims=True)
        probs_low = probs.astype(jnp.bfloat16)
        prob_grad = jnp.einsum(
            "pbkgd,pjkd->pkgbj", grad_now, neighbor_values, preferred_element_type=jnp.float32
        )
        row_dot = jnp.sum(probs * prob_grad, axis=-1, keepdims=True)
        score_grad = (probs * (prob_grad - row_dot)).astype(jnp.bfloat16)
        query_grad = (
            jnp.einsum(
                "pkgbj,pjkd->pbkgd", score_grad, neighbor_keys, preferred_element_type=jnp.float32
            )
            * scale_factor
        )
        key_part = (
            jnp.einsum(
                "pkgbj,pbkgd->pjkd", score_grad, query_now, preferred_element_type=jnp.float32
            )
            * scale_factor
        )
        value_part = jnp.einsum(
            "pkgbj,pbkgd->pjkd", probs_low, grad_now, preferred_element_type=jnp.float32
        )
        query_grad = query_grad.reshape(turn_rows, local_width)
        gain_part = jnp.sum(input_now.astype(jnp.float32) * query_grad, axis=0)
        return (
            query_grad,
            key_part.reshape(per_turn, listed * block_rows, slot_width),
            value_part.reshape(per_turn, listed * block_rows, slot_width),
            gain_part,
        )

    def spare(unit, head_grad):
        empty_part = jnp.zeros((per_turn, listed * block_rows, slot_width), jnp.float32)
        return (
            jnp.zeros((turn_rows, local_width), jnp.float32),
            empty_part,
            empty_part,
            jnp.zeros((local_width,), jnp.float32),
        )

    on_top = section_pos == section_count - 1

    def turn_step(turn, carry):
        incoming, result_heads, key_slots, value_slots, gain_acc = carry
        unit = turn - (section_count - 1 - section_pos)
        active = (unit >= 0) & (unit < unit_count)
        safe_index = jnp.clip(unit, 0, unit_count - 1)
        target = jnp.where(active, safe_index, unit_count)
        from_top = lax.dynamic_slice_in_dim(head_top, safe_index * turn_rows, turn_rows, 0)
        head_grad = jnp.where(on_top, from_top, incoming)
        query_grad, key_part, value_part, gain_part = lax.cond(
            active, attend, spare, safe_index, head_grad
        )
        moved_grad = (gain_row * query_grad).astype(jnp.bfloat16)
        handed = (head_grad.astype(jnp.float32) + moved_grad.astype(jnp.float32)).astype(
            jnp.bfloat16
        )
        result_heads = lax.dynamic_update_slice_in_dim(result_heads, handed, target * turn_rows, 0)
        key_slots = lax.dynamic_update_slice_in_dim(key_slots, key_part, target * per_turn, 0)
        value_slots = lax.dynamic_update_slice_in_dim(value_slots, value_part, target * per_turn, 0)
        gain_acc = gain_acc + gain_part
        incoming = passed_along(handed, "section", -1)
        return (incoming, result_heads, key_slots, value_slots, gain_acc)

    first_incoming = jnp.zeros((turn_rows, local_width), jnp.bfloat16)
    slot_zeros = jnp.zeros(
        ((unit_count + 1) * per_turn, listed * block_rows, slot_width), jnp.float32
    )
    start_carry = (
        first_incoming,
        jnp.zeros(((unit_count + 1) * turn_rows, local_width), jnp.bfloat16),
        slot_zeros,
        slot_zeros,
        jnp.zeros((local_width,), jnp.float32),
    )
    final_carry = lax.fori_loop(0, turn_count, turn_step, start_carry)
    incoming, result_heads, key_slots, value_slots, gain_acc = final_carry
    result_rows = lax.all_to_all(
        result_heads[:total_rows], "ctx", split_axis=0, concat_axis=1, tiled=True
    )
    target_labels = block_lists.reshape(-1)
    key_pieces = key_slots[:block_count].reshape(block_count * listed, block_rows, slot_width)
    value_pieces = value_slots[:block_count].reshape(block_count * listed, block_rows, slot_width)
    key_acc = (
        jnp.zeros((block_count, block_rows, slot_width), jnp.float32)
        .at[target_labels]
        .add(key_pieces)
    )
    value_acc = (
        jnp.zeros((block_count, block_rows, slot_width), jnp.float32)
        .at[target_labels]
        .add(value_pieces)
    )
    key_back, value_back = (
        lax.all_to_all(
            key_acc.reshape(total_rows, slot_width).astype(jnp.bfloat16),
            "ctx",
            split_axis=0,
            concat_axis=1,
            tiled=True,
        ).astype(jnp.float32),
        lax.all_to_all(
            value_acc.reshape(total_rows, slot_width).astype(jnp.bfloat16),
            "ctx",
            split_axis=0,
            concat_axis=1,
            tiled=True,
        ).astype(jnp.float32),
    )
    key_out = (
        key_back.reshape(tok_local, kv_heads, repeats, HEAD_FEATURES)
        .sum(axis=2)
        .reshape(tok_local, kv_width)
        .astype(jnp.bfloat16)
    )
    value_out = (
        value_back.reshape(tok_local, kv_heads, repeats, HEAD_FEATURES)
        .sum(axis=2)
        .reshape(tok_local, kv_width)
        .astype(jnp.bfloat16)
    )
    gain_total = lax.psum(gain_acc, "dp")
    return (result_rows[None, None], key_out[None, None], value_out[None, None], gain_total[None])


def solution(mesh):
    placed = (
        P("section", "dp", "ctx", None),
        P("section", "dp", "ctx", None),
        P("section", "dp", "ctx", None),
        P("section", "ctx"),
        P("dp", "ctx", None),
        P(),
    )
    return jax.shard_map(
        shards,
        mesh=mesh,
        in_specs=placed,
        out_specs=(
            P("section", "dp", "ctx", None),
            P("section", "dp", "ctx", None),
            P("section", "dp", "ctx", None),
            P("section", "ctx"),
        ),
        check_vma=False,
    )
```

```python
import math

import jax
import jax.numpy as jnp
import numpy as np
from jax import lax
from jax.sharding import PartitionSpec as P

HEAD_FEATURES = 128


def passed_along(block, axis, distance):
    devices = range(lax.axis_size(axis))
    route = [(i - distance, i) for i in devices if i - distance in devices]
    return lax.ppermute(block, axis, route)


def shards(query_input, key_states, value_states, query_gain, top_grad, block_lists):
    ctx_count = lax.axis_size("ctx")
    section_count = lax.axis_size("section")
    section_pos = lax.axis_index("section")
    layer_input = query_input[0, 0]
    tok_local, feature_count = layer_input.shape
    kv_width = key_states.shape[-1]
    kv_heads = kv_width // HEAD_FEATURES
    head_count = feature_count // HEAD_FEATURES
    local_heads = head_count // ctx_count
    group_width = head_count // kv_heads
    local_kv = max(1, local_heads // group_width)
    per_kv = local_heads // local_kv
    repeats = ctx_count * local_kv // kv_heads
    local_width = local_heads * HEAD_FEATURES
    slot_width = local_kv * HEAD_FEATURES
    total_rows = tok_local * ctx_count
    block_count, listed = block_lists.shape
    block_rows = total_rows // block_count
    scale_factor = 1.0 / math.sqrt(HEAD_FEATURES)
    slot_index = np.arange(ctx_count * local_kv)
    slot_heads = slot_index // local_kv * local_heads // group_width + slot_index % local_kv
    sent_keys = (
        key_states[0, 0]
        .reshape(tok_local, kv_heads, HEAD_FEATURES)[:, slot_heads]
        .reshape(tok_local, ctx_count * slot_width)
    )
    sent_values = (
        value_states[0, 0]
        .reshape(tok_local, kv_heads, HEAD_FEATURES)[:, slot_heads]
        .reshape(tok_local, ctx_count * slot_width)
    )
    sent_widths = (local_width, local_width, slot_width, slot_width)
    packed = jnp.concatenate(
        [
            piece.reshape(tok_local, ctx_count, width)
            for piece, width in zip(
                (layer_input, top_grad[0], sent_keys, sent_values), sent_widths
            )
        ],
        axis=2,
    ).reshape(tok_local, ctx_count * sum(sent_widths))
    moved = lax.all_to_all(packed, "ctx", split_axis=1, concat_axis=0, tiled=True)
    edges = np.cumsum((0,) + sent_widths)
    head_input, head_top, head_keys, head_values = (
        moved[:, edges[i] : edges[i + 1]] for i in range(len(sent_widths))
    )
    gain_row = query_gain[0]
    query_rows = (head_input.astype(jnp.float32) * gain_row).astype(jnp.bfloat16)
    blocked_keys = head_keys.reshape(block_count, block_rows, local_kv, HEAD_FEATURES)
    blocked_values = head_values.reshape(block_count, block_rows, local_kv, HEAD_FEATURES)
    per_turn = 2
    unit_count = block_count // per_turn
    turn_rows = per_turn * block_rows
    token_rows = turn_rows // ctx_count
    turn_count = unit_count + section_count - 1
    grid_shape = (per_turn, block_rows, local_kv, per_kv, HEAD_FEATURES)

    def attend(unit, head_grad):
        first_row = unit * turn_rows
        query_now = lax.dynamic_slice_in_dim(query_rows, first_row, turn_rows, 0).reshape(
            grid_shape
        )
        input_now = lax.dynamic_slice_in_dim(head_input, first_row, turn_rows, 0)
        grad_now = head_grad.reshape(grid_shape)
        lists_now = lax.dynamic_slice_in_dim(block_lists, unit * per_turn, per_turn, 0)
        neighbor_keys = blocked_keys[lists_now].reshape(
            per_turn, listed * block_rows, local_kv, HEAD_FEATURES
        )
        neighbor_values = blocked_values[lists_now].reshape(
            per_turn, listed * block_rows, local_kv, HEAD_FEATURES
        )
        scores = (
            jnp.einsum(
                "pbkgd,pjkd->pkgbj", query_now, neighbor_keys, preferred_element_type=jnp.float32
            )
            * scale_factor
        )
        row_max = jnp.max(scores, axis=-1, keepdims=True)
        weights = jnp.exp(scores - row_max)
        probs = weights / jnp.sum(weights, axis=-1, keepdims=True)
        probs_low = probs.astype(jnp.bfloat16)
        prob_grad = jnp.einsum(
            "pbkgd,pjkd->pkgbj", grad_now, neighbor_values, preferred_element_type=jnp.float32
        )
        row_dot = jnp.sum(probs * prob_grad, axis=-1, keepdims=True)
        score_grad = (probs * (prob_grad - row_dot)).astype(jnp.bfloat16)
        query_grad = (
            jnp.einsum(
                "pkgbj,pjkd->pbkgd", score_grad, neighbor_keys, preferred_element_type=jnp.float32
            )
            * scale_factor
        )
        key_part = (
            jnp.einsum(
                "pkgbj,pbkgd->pjkd", score_grad, query_now, preferred_element_type=jnp.float32
            )
            * scale_factor
        )
        value_part = jnp.einsum(
            "pkgbj,pbkgd->pjkd", probs_low, grad_now, preferred_element_type=jnp.float32
        )
        query_grad = query_grad.reshape(turn_rows, local_width)
        gain_part = jnp.sum(input_now.astype(jnp.float32) * query_grad, axis=0)
        return (
            query_grad,
            key_part.reshape(per_turn, listed * block_rows, slot_width),
            value_part.reshape(per_turn, listed * block_rows, slot_width),
            gain_part,
        )

    def spare(unit, head_grad):
        empty_part = jnp.zeros((per_turn, listed * block_rows, slot_width), jnp.float32)
        return (
            jnp.zeros((turn_rows, local_width), jnp.float32),
            empty_part,
            empty_part,
            jnp.zeros((local_width,), jnp.float32),
        )

    on_top = section_pos == section_count - 1

    def turn_step(turn, carry):
        incoming, result_heads, key_slots, value_slots, gain_acc = carry
        unit = turn - (section_count - 1 - section_pos)
        active = (unit >= 0) & (unit < unit_count)
        safe_index = jnp.clip(unit, 0, unit_count - 1)
        from_top = lax.dynamic_slice_in_dim(head_top, safe_index * turn_rows, turn_rows, 0)
        head_grad = jnp.where(on_top, from_top, incoming)
        query_grad, key_part, value_part, gain_part = lax.cond(
            active, attend, spare, safe_index, head_grad
        )
        moved_grad = (gain_row * query_grad).astype(jnp.bfloat16)
        handed = (head_grad.astype(jnp.float32) + moved_grad.astype(jnp.float32)).astype(
            jnp.bfloat16
        )
        def kept(array, part, size):
            start = safe_index * size
            old = lax.dynamic_slice_in_dim(array, start, size, 0)
            return lax.dynamic_update_slice_in_dim(array, jnp.where(active, part, old), start, 0)

        result_heads = kept(result_heads, handed, turn_rows)
        key_slots = kept(key_slots, key_part, per_turn)
        value_slots = kept(value_slots, value_part, per_turn)
        gain_acc = gain_acc + gain_part
        incoming = passed_along(handed, "section", -1)
        return (incoming, result_heads, key_slots, value_slots, gain_acc)

    first_incoming = jnp.zeros((turn_rows, local_width), jnp.bfloat16)
    slot_zeros = jnp.zeros((unit_count * per_turn, listed * block_rows, slot_width), jnp.float32)
    start_carry = (
        first_incoming,
        jnp.zeros((unit_count * turn_rows, local_width), jnp.bfloat16),
        slot_zeros,
        slot_zeros,
        jnp.zeros((local_width,), jnp.float32),
    )
    final_carry = lax.fori_loop(0, turn_count, turn_step, start_carry)
    incoming, result_heads, key_slots, value_slots, gain_acc = final_carry
    target_labels = block_lists.reshape(-1)
    key_pieces = key_slots.reshape(block_count * listed, block_rows, slot_width)
    value_pieces = value_slots.reshape(block_count * listed, block_rows, slot_width)
    key_acc = (
        jnp.zeros((block_count, block_rows, slot_width), jnp.float32)
        .at[target_labels]
        .add(key_pieces)
    )
    value_acc = (
        jnp.zeros((block_count, block_rows, slot_width), jnp.float32)
        .at[target_labels]
        .add(value_pieces)
    )
    back_widths = (local_width, slot_width, slot_width)
    sent_back = jnp.concatenate(
        [
            result_heads,
            key_acc.reshape(total_rows, slot_width).astype(jnp.bfloat16),
            value_acc.reshape(total_rows, slot_width).astype(jnp.bfloat16),
        ],
        axis=1,
    )
    came_back = lax.all_to_all(
        sent_back, "ctx", split_axis=0, concat_axis=1, tiled=True
    ).reshape(tok_local, ctx_count, sum(back_widths))
    back_edges = np.cumsum((0,) + back_widths)
    result_rows, key_back, value_back = (
        came_back[:, :, back_edges[i] : back_edges[i + 1]].reshape(tok_local, -1)
        for i in range(len(back_widths))
    )
    key_out = (
        key_back.astype(jnp.float32)
        .reshape(tok_local, kv_heads, repeats, HEAD_FEATURES)
        .sum(axis=2)
        .reshape(tok_local, kv_width)
        .astype(jnp.bfloat16)
    )
    value_out = (
        value_back.astype(jnp.float32)
        .reshape(tok_local, kv_heads, repeats, HEAD_FEATURES)
        .sum(axis=2)
        .reshape(tok_local, kv_width)
        .astype(jnp.bfloat16)
    )
    gain_total = lax.psum(gain_acc, "dp")
    return (result_rows[None, None], key_out[None, None], value_out[None, None], gain_total[None])


def solution(mesh):
    placed = (
        P("section", "dp", "ctx", None),
        P("section", "dp", "ctx", None),
        P("section", "dp", "ctx", None),
        P("section", "ctx"),
        P("dp", "ctx", None),
        P(),
    )
    return jax.shard_map(
        shards,
        mesh=mesh,
        in_specs=placed,
        out_specs=(
            P("section", "dp", "ctx", None),
            P("section", "dp", "ctx", None),
            P("section", "dp", "ctx", None),
            P("section", "ctx"),
        ),
        check_vma=False,
    )
```

```python
import math

import jax
import jax.numpy as jnp
import numpy as np
from jax import lax
from jax.sharding import PartitionSpec as P

HEAD_FEATURES = 128


def passed_along(block, axis, distance):
    devices = range(lax.axis_size(axis))
    route = [(i - distance, i) for i in devices if i - distance in devices]
    return lax.ppermute(block, axis, route)


def shards(query_input, key_states, value_states, query_gain, top_grad, block_lists):
    ctx_count = lax.axis_size("ctx")
    section_count = lax.axis_size("section")
    section_pos = lax.axis_index("section")
    layer_input = query_input[0, 0]
    tok_local, feature_count = layer_input.shape
    kv_width = key_states.shape[-1]
    kv_heads = kv_width // HEAD_FEATURES
    head_count = feature_count // HEAD_FEATURES
    local_heads = head_count // ctx_count
    group_width = head_count // kv_heads
    local_kv = max(1, local_heads // group_width)
    per_kv = local_heads // local_kv
    repeats = ctx_count * local_kv // kv_heads
    local_width = local_heads * HEAD_FEATURES
    slot_width = local_kv * HEAD_FEATURES
    total_rows = tok_local * ctx_count
    block_count, listed = block_lists.shape
    block_rows = total_rows // block_count
    scale_factor = 1.0 / math.sqrt(HEAD_FEATURES)
    slot_index = np.arange(ctx_count * local_kv)
    slot_heads = slot_index // local_kv * local_heads // group_width + slot_index % local_kv
    sent_keys = (
        key_states[0, 0]
        .reshape(tok_local, kv_heads, HEAD_FEATURES)[:, slot_heads]
        .reshape(tok_local, ctx_count * slot_width)
    )
    sent_values = (
        value_states[0, 0]
        .reshape(tok_local, kv_heads, HEAD_FEATURES)[:, slot_heads]
        .reshape(tok_local, ctx_count * slot_width)
    )
    sent_widths = (local_width, local_width, slot_width, slot_width)
    packed = jnp.concatenate(
        [
            piece.reshape(tok_local, ctx_count, width)
            for piece, width in zip(
                (layer_input, top_grad[0], sent_keys, sent_values), sent_widths
            )
        ],
        axis=2,
    ).reshape(tok_local, ctx_count * sum(sent_widths))
    moved = lax.all_to_all(packed, "ctx", split_axis=1, concat_axis=0, tiled=True)
    edges = np.cumsum((0,) + sent_widths)
    head_input, head_top, head_keys, head_values = lax.optimization_barrier(
        tuple(moved[:, edges[i] : edges[i + 1]] for i in range(len(sent_widths)))
    )
    gain_row = query_gain[0]
    query_rows = (head_input.astype(jnp.float32) * gain_row).astype(jnp.bfloat16)
    blocked_keys = head_keys.reshape(block_count, block_rows, local_kv, HEAD_FEATURES)
    blocked_values = head_values.reshape(block_count, block_rows, local_kv, HEAD_FEATURES)
    per_turn = 2
    unit_count = block_count // per_turn
    turn_rows = per_turn * block_rows
    token_rows = turn_rows // ctx_count
    turn_count = unit_count + section_count - 1
    grid_shape = (per_turn, block_rows, local_kv, per_kv, HEAD_FEATURES)

    def attend(unit, head_grad):
        first_row = unit * turn_rows
        query_now = lax.dynamic_slice_in_dim(query_rows, first_row, turn_rows, 0).reshape(
            grid_shape
        )
        input_now = lax.dynamic_slice_in_dim(head_input, first_row, turn_rows, 0)
        grad_now = head_grad.reshape(grid_shape)
        lists_now = lax.dynamic_slice_in_dim(block_lists, unit * per_turn, per_turn, 0)
        neighbor_keys = blocked_keys[lists_now].reshape(
            per_turn, listed * block_rows, local_kv, HEAD_FEATURES
        )
        neighbor_values = blocked_values[lists_now].reshape(
            per_turn, listed * block_rows, local_kv, HEAD_FEATURES
        )
        scores = (
            jnp.einsum(
                "pbkgd,pjkd->pkgbj", query_now, neighbor_keys, preferred_element_type=jnp.float32
            )
            * scale_factor
        )
        row_max = jnp.max(scores, axis=-1, keepdims=True)
        weights = jnp.exp(scores - row_max)
        probs = weights / jnp.sum(weights, axis=-1, keepdims=True)
        probs_low = probs.astype(jnp.bfloat16)
        prob_grad = jnp.einsum(
            "pbkgd,pjkd->pkgbj", grad_now, neighbor_values, preferred_element_type=jnp.float32
        )
        row_dot = jnp.sum(probs * prob_grad, axis=-1, keepdims=True)
        score_grad = (probs * (prob_grad - row_dot)).astype(jnp.bfloat16)
        query_grad = (
            jnp.einsum(
                "pkgbj,pjkd->pbkgd", score_grad, neighbor_keys, preferred_element_type=jnp.float32
            )
            * scale_factor
        )
        key_part = (
            jnp.einsum(
                "pkgbj,pbkgd->pjkd", score_grad, query_now, preferred_element_type=jnp.float32
            )
            * scale_factor
        )
        value_part = jnp.einsum(
            "pkgbj,pbkgd->pjkd", probs_low, grad_now, preferred_element_type=jnp.float32
        )
        query_grad = query_grad.reshape(turn_rows, local_width)
        gain_part = jnp.sum(input_now.astype(jnp.float32) * query_grad, axis=0)
        return (
            query_grad,
            key_part.reshape(per_turn, listed * block_rows, slot_width),
            value_part.reshape(per_turn, listed * block_rows, slot_width),
            gain_part,
        )

    def spare(unit, head_grad):
        empty_part = jnp.zeros((per_turn, listed * block_rows, slot_width), jnp.float32)
        return (
            jnp.zeros((turn_rows, local_width), jnp.float32),
            empty_part,
            empty_part,
            jnp.zeros((local_width,), jnp.float32),
        )

    on_top = section_pos == section_count - 1

    def turn_step(turn, carry):
        incoming, result_heads, key_slots, value_slots, gain_acc = carry
        unit = turn - (section_count - 1 - section_pos)
        active = (unit >= 0) & (unit < unit_count)
        safe_index = jnp.clip(unit, 0, unit_count - 1)
        target = jnp.where(active, safe_index, unit_count)
        from_top = lax.dynamic_slice_in_dim(head_top, safe_index * turn_rows, turn_rows, 0)
        head_grad = jnp.where(on_top, from_top, incoming)
        query_grad, key_part, value_part, gain_part = lax.cond(
            active, attend, spare, safe_index, head_grad
        )
        moved_grad = (gain_row * query_grad).astype(jnp.bfloat16)
        handed = (head_grad.astype(jnp.float32) + moved_grad.astype(jnp.float32)).astype(
            jnp.bfloat16
        )
        result_heads = lax.dynamic_update_slice_in_dim(result_heads, handed, target * turn_rows, 0)
        key_slots = lax.dynamic_update_slice_in_dim(key_slots, key_part, target * per_turn, 0)
        value_slots = lax.dynamic_update_slice_in_dim(value_slots, value_part, target * per_turn, 0)
        gain_acc = gain_acc + gain_part
        incoming = passed_along(handed, "section", -1)
        return (incoming, result_heads, key_slots, value_slots, gain_acc)

    first_incoming = jnp.zeros((turn_rows, local_width), jnp.bfloat16)
    slot_zeros = jnp.zeros(
        ((unit_count + 1) * per_turn, listed * block_rows, slot_width), jnp.float32
    )
    start_carry = (
        first_incoming,
        jnp.zeros(((unit_count + 1) * turn_rows, local_width), jnp.bfloat16),
        slot_zeros,
        slot_zeros,
        jnp.zeros((local_width,), jnp.float32),
    )
    final_carry = lax.fori_loop(0, turn_count, turn_step, start_carry)
    incoming, result_heads, key_slots, value_slots, gain_acc = final_carry
    result_rows = lax.all_to_all(
        result_heads[:total_rows], "ctx", split_axis=0, concat_axis=1, tiled=True
    )
    target_labels = block_lists.reshape(-1)
    key_pieces = key_slots[:block_count].reshape(block_count * listed, block_rows, slot_width)
    value_pieces = value_slots[:block_count].reshape(block_count * listed, block_rows, slot_width)
    key_acc = (
        jnp.zeros((block_count, block_rows, slot_width), jnp.float32)
        .at[target_labels]
        .add(key_pieces)
    )
    value_acc = (
        jnp.zeros((block_count, block_rows, slot_width), jnp.float32)
        .at[target_labels]
        .add(value_pieces)
    )
    key_back, value_back = (
        lax.all_to_all(
            key_acc.reshape(total_rows, slot_width).astype(jnp.bfloat16),
            "ctx",
            split_axis=0,
            concat_axis=1,
            tiled=True,
        ).astype(jnp.float32),
        lax.all_to_all(
            value_acc.reshape(total_rows, slot_width).astype(jnp.bfloat16),
            "ctx",
            split_axis=0,
            concat_axis=1,
            tiled=True,
        ).astype(jnp.float32),
    )
    key_out = (
        key_back.reshape(tok_local, kv_heads, repeats, HEAD_FEATURES)
        .sum(axis=2)
        .reshape(tok_local, kv_width)
        .astype(jnp.bfloat16)
    )
    value_out = (
        value_back.reshape(tok_local, kv_heads, repeats, HEAD_FEATURES)
        .sum(axis=2)
        .reshape(tok_local, kv_width)
        .astype(jnp.bfloat16)
    )
    gain_total = lax.psum(gain_acc, "dp")
    return (result_rows[None, None], key_out[None, None], value_out[None, None], gain_total[None])


def solution(mesh):
    placed = (
        P("section", "dp", "ctx", None),
        P("section", "dp", "ctx", None),
        P("section", "dp", "ctx", None),
        P("section", "ctx"),
        P("dp", "ctx", None),
        P(),
    )
    return jax.shard_map(
        shards,
        mesh=mesh,
        in_specs=placed,
        out_specs=(
            P("section", "dp", "ctx", None),
            P("section", "dp", "ctx", None),
            P("section", "dp", "ctx", None),
            P("section", "ctx"),
        ),
        check_vma=False,
    )
```

```python
import math

import jax
import jax.numpy as jnp
import numpy as np
from jax import lax
from jax.sharding import PartitionSpec as P

HEAD_FEATURES = 128


def passed_along(block, axis, distance):
    devices = range(lax.axis_size(axis))
    route = [(i - distance, i) for i in devices if i - distance in devices]
    return lax.ppermute(block, axis, route)


def shards(query_input, key_states, value_states, query_gain, top_grad, block_lists):
    ctx_count = lax.axis_size("ctx")
    section_count = lax.axis_size("section")
    section_pos = lax.axis_index("section")
    layer_input = query_input[0, 0]
    tok_local, feature_count = layer_input.shape
    kv_width = key_states.shape[-1]
    kv_heads = kv_width // HEAD_FEATURES
    head_count = feature_count // HEAD_FEATURES
    local_heads = head_count // ctx_count
    group_width = head_count // kv_heads
    local_kv = max(1, local_heads // group_width)
    per_kv = local_heads // local_kv
    repeats = ctx_count * local_kv // kv_heads
    local_width = local_heads * HEAD_FEATURES
    slot_width = local_kv * HEAD_FEATURES
    total_rows = tok_local * ctx_count
    block_count, listed = block_lists.shape
    block_rows = total_rows // block_count
    scale_factor = 1.0 / math.sqrt(HEAD_FEATURES)
    slot_index = np.arange(ctx_count * local_kv)
    slot_heads = slot_index // local_kv * local_heads // group_width + slot_index % local_kv
    sent_keys = (
        key_states[0, 0]
        .reshape(tok_local, kv_heads, HEAD_FEATURES)[:, slot_heads]
        .reshape(tok_local, ctx_count * slot_width)
    )
    sent_values = (
        value_states[0, 0]
        .reshape(tok_local, kv_heads, HEAD_FEATURES)[:, slot_heads]
        .reshape(tok_local, ctx_count * slot_width)
    )
    sent_widths = (local_width, local_width, slot_width, slot_width)
    packed = jnp.concatenate(
        [
            piece.reshape(tok_local, ctx_count, width)
            for piece, width in zip(
                (layer_input, top_grad[0], sent_keys, sent_values), sent_widths
            )
        ],
        axis=2,
    ).reshape(tok_local, ctx_count * sum(sent_widths))
    moved = lax.all_to_all(packed, "ctx", split_axis=1, concat_axis=0, tiled=True)
    edges = np.cumsum((0,) + sent_widths)
    head_input, head_top, head_keys, head_values = lax.optimization_barrier(
        tuple(moved[:, edges[i] : edges[i + 1]] for i in range(len(sent_widths)))
    )
    gain_row = query_gain[0]
    query_rows = (head_input.astype(jnp.float32) * gain_row).astype(jnp.bfloat16)
    blocked_keys = head_keys.reshape(block_count, block_rows, local_kv, HEAD_FEATURES)
    blocked_values = head_values.reshape(block_count, block_rows, local_kv, HEAD_FEATURES)
    per_turn = 4
    unit_count = block_count // per_turn
    turn_rows = per_turn * block_rows
    token_rows = turn_rows // ctx_count
    turn_count = unit_count + section_count - 1
    grid_shape = (per_turn, block_rows, local_kv, per_kv, HEAD_FEATURES)

    def attend(unit, head_grad):
        first_row = unit * turn_rows
        query_now = lax.dynamic_slice_in_dim(query_rows, first_row, turn_rows, 0).reshape(
            grid_shape
        )
        input_now = lax.dynamic_slice_in_dim(head_input, first_row, turn_rows, 0)
        grad_now = head_grad.reshape(grid_shape)
        lists_now = lax.dynamic_slice_in_dim(block_lists, unit * per_turn, per_turn, 0)
        neighbor_keys = blocked_keys[lists_now].reshape(
            per_turn, listed * block_rows, local_kv, HEAD_FEATURES
        )
        neighbor_values = blocked_values[lists_now].reshape(
            per_turn, listed * block_rows, local_kv, HEAD_FEATURES
        )
        scores = (
            jnp.einsum(
                "pbkgd,pjkd->pkgbj", query_now, neighbor_keys, preferred_element_type=jnp.float32
            )
            * scale_factor
        )
        row_max = jnp.max(scores, axis=-1, keepdims=True)
        weights = jnp.exp(scores - row_max)
        probs = weights / jnp.sum(weights, axis=-1, keepdims=True)
        probs_low = probs.astype(jnp.bfloat16)
        prob_grad = jnp.einsum(
            "pbkgd,pjkd->pkgbj", grad_now, neighbor_values, preferred_element_type=jnp.float32
        )
        row_dot = jnp.sum(probs * prob_grad, axis=-1, keepdims=True)
        score_grad = (probs * (prob_grad - row_dot)).astype(jnp.bfloat16)
        query_grad = (
            jnp.einsum(
                "pkgbj,pjkd->pbkgd", score_grad, neighbor_keys, preferred_element_type=jnp.float32
            )
            * scale_factor
        )
        key_part = (
            jnp.einsum(
                "pkgbj,pbkgd->pjkd", score_grad, query_now, preferred_element_type=jnp.float32
            )
            * scale_factor
        )
        value_part = jnp.einsum(
            "pkgbj,pbkgd->pjkd", probs_low, grad_now, preferred_element_type=jnp.float32
        )
        query_grad = query_grad.reshape(turn_rows, local_width)
        gain_part = jnp.sum(input_now.astype(jnp.float32) * query_grad, axis=0)
        return (
            query_grad,
            key_part.reshape(per_turn, listed * block_rows, slot_width),
            value_part.reshape(per_turn, listed * block_rows, slot_width),
            gain_part,
        )

    def spare(unit, head_grad):
        empty_part = jnp.zeros((per_turn, listed * block_rows, slot_width), jnp.float32)
        return (
            jnp.zeros((turn_rows, local_width), jnp.float32),
            empty_part,
            empty_part,
            jnp.zeros((local_width,), jnp.float32),
        )

    on_top = section_pos == section_count - 1

    def turn_step(turn, carry):
        incoming, result_heads, key_slots, value_slots, gain_acc = carry
        unit = turn - (section_count - 1 - section_pos)
        active = (unit >= 0) & (unit < unit_count)
        safe_index = jnp.clip(unit, 0, unit_count - 1)
        target = jnp.where(active, safe_index, unit_count)
        from_top = lax.dynamic_slice_in_dim(head_top, safe_index * turn_rows, turn_rows, 0)
        head_grad = jnp.where(on_top, from_top, incoming)
        query_grad, key_part, value_part, gain_part = lax.cond(
            active, attend, spare, safe_index, head_grad
        )
        moved_grad = (gain_row * query_grad).astype(jnp.bfloat16)
        handed = (head_grad.astype(jnp.float32) + moved_grad.astype(jnp.float32)).astype(
            jnp.bfloat16
        )
        result_heads = lax.dynamic_update_slice_in_dim(result_heads, handed, target * turn_rows, 0)
        key_slots = lax.dynamic_update_slice_in_dim(key_slots, key_part, target * per_turn, 0)
        value_slots = lax.dynamic_update_slice_in_dim(value_slots, value_part, target * per_turn, 0)
        gain_acc = gain_acc + gain_part
        incoming = passed_along(handed, "section", -1)
        return (incoming, result_heads, key_slots, value_slots, gain_acc)

    first_incoming = jnp.zeros((turn_rows, local_width), jnp.bfloat16)
    slot_count = (unit_count + 1) * per_turn
    slot_zeros = jnp.zeros((slot_count, listed * block_rows, slot_width), jnp.float32)
    start_carry = (
        first_incoming,
        jnp.zeros(((unit_count + 1) * turn_rows, local_width), jnp.bfloat16),
        slot_zeros,
        slot_zeros,
        jnp.zeros((local_width,), jnp.float32),
    )
    final_carry = lax.fori_loop(0, turn_count, turn_step, start_carry)
    incoming, result_heads, key_slots, value_slots, gain_acc = final_carry
    result_rows = lax.all_to_all(
        result_heads[:total_rows], "ctx", split_axis=0, concat_axis=1, tiled=True
    )
    spare_labels = jnp.full(((slot_count - block_count) * listed,), -1, block_lists.dtype)
    target_labels = jnp.concatenate([block_lists.reshape(-1), spare_labels])
    pick = (target_labels[None, :] == jnp.arange(block_count)[:, None]).astype(jnp.float32)

    def gathered(slots):
        return jnp.dot(
            pick,
            slots.reshape(slot_count * listed, block_rows * slot_width),
            precision=lax.Precision.HIGHEST,
        )

    key_acc = gathered(key_slots)
    value_acc = gathered(value_slots)
    key_back, value_back = (
        lax.all_to_all(
            key_acc.reshape(total_rows, slot_width).astype(jnp.bfloat16),
            "ctx",
            split_axis=0,
            concat_axis=1,
            tiled=True,
        ).astype(jnp.float32),
        lax.all_to_all(
            value_acc.reshape(total_rows, slot_width).astype(jnp.bfloat16),
            "ctx",
            split_axis=0,
            concat_axis=1,
            tiled=True,
        ).astype(jnp.float32),
    )
    key_out = (
        key_back.reshape(tok_local, kv_heads, repeats, HEAD_FEATURES)
        .sum(axis=2)
        .reshape(tok_local, kv_width)
        .astype(jnp.bfloat16)
    )
    value_out = (
        value_back.reshape(tok_local, kv_heads, repeats, HEAD_FEATURES)
        .sum(axis=2)
        .reshape(tok_local, kv_width)
        .astype(jnp.bfloat16)
    )
    gain_total = lax.psum(gain_acc, "dp")
    return (result_rows[None, None], key_out[None, None], value_out[None, None], gain_total[None])


def solution(mesh):
    placed = (
        P("section", "dp", "ctx", None),
        P("section", "dp", "ctx", None),
        P("section", "dp", "ctx", None),
        P("section", "ctx"),
        P("dp", "ctx", None),
        P(),
    )
    return jax.shard_map(
        shards,
        mesh=mesh,
        in_specs=placed,
        out_specs=(
            P("section", "dp", "ctx", None),
            P("section", "dp", "ctx", None),
            P("section", "dp", "ctx", None),
            P("section", "ctx"),
        ),
        check_vma=False,
    )
```

```python
import math

import jax
import jax.numpy as jnp
from jax import lax
from jax.sharding import PartitionSpec as P

HEAD_FEATURES = 128


def passed_along(block, axis, distance):
    devices = range(lax.axis_size(axis))
    route = [(i - distance, i) for i in devices if i - distance in devices]
    return lax.ppermute(block, axis, route)


def cyclic_shift(block, axis, distance):
    count = lax.axis_size(axis)
    return lax.ppermute(block, axis, [(i, (i + distance) % count) for i in range(count)])


def shards(query_input, key_states, value_states, query_gain, top_grad, block_lists):
    ctx_count = lax.axis_size("ctx")
    section_count = lax.axis_size("section")
    section_pos = lax.axis_index("section")
    ctx_pos = lax.axis_index("ctx")
    layer_input = query_input[0, 0]
    tok_local, feature_count = layer_input.shape
    kv_width = key_states.shape[-1]
    kv_heads = kv_width // HEAD_FEATURES
    head_count = feature_count // HEAD_FEATURES
    group_width = head_count // kv_heads
    group_features = group_width * HEAD_FEATURES
    gain_width = query_gain.shape[-1]
    block_count, listed = block_lists.shape
    block_rows = tok_local
    assert block_count == ctx_count and listed == 4
    scale_factor = 1.0 / math.sqrt(HEAD_FEATURES)
    turn_count = kv_heads + section_count - 1
    last = ctx_count - 1

    first_row = block_lists[0]
    first_extra = jnp.sum(
        jnp.where((first_row != last) & (first_row != 0) & (first_row != 1), first_row, 0)
    )
    last_row = block_lists[last]
    last_extra = jnp.sum(
        jnp.where((last_row != last - 1) & (last_row != last) & (last_row != 0), last_row, 0)
    )
    is_first = ctx_pos == 0
    is_last = ctx_pos == last
    is_second = ctx_pos == 1
    uses_zero = ~(is_first | is_last | is_second)
    lane_sources = jnp.stack([ctx_pos == 0, ctx_pos == first_extra, ctx_pos == last_extra, is_last])
    lane_users = jnp.stack([uses_zero, is_first, is_last, is_second])

    gain_placed = jnp.zeros((feature_count,), jnp.float32)
    gain_placed = lax.dynamic_update_slice_in_dim(
        gain_placed, query_gain[0], ctx_pos * gain_width, 0
    )
    own_kv = jnp.stack([key_states[0, 0], value_states[0, 0]])
    lanes_out = jnp.where(lane_sources[:, None, None, None], own_kv[None], jnp.zeros_like(own_kv)[None])
    lanes_in = lax.psum(lanes_out, "ctx")
    gain_row = lax.psum(gain_placed, "ctx")
    extra_kv = jnp.sum(
        jnp.where(lane_users[:, None, None, None], lanes_in, jnp.zeros_like(lanes_in)), axis=0
    )
    prev_kv = cyclic_shift(own_kv, "ctx", 1)
    next_kv = cyclic_shift(own_kv, "ctx", -1)
    pool_kv = jnp.stack([prev_kv, own_kv, next_kv, extra_kv], axis=1)

    query_rows = (layer_input.astype(jnp.float32) * gain_row).astype(jnp.bfloat16)
    own_top = top_grad[0]
    on_top = section_pos == section_count - 1
    lag = section_count - 1 - section_pos

    def group_cols(array, group, width):
        return lax.dynamic_slice_in_dim(array, group * width, width, array.ndim - 1)

    def attend(group, head_grad):
        pool = group_cols(pool_kv, group, HEAD_FEATURES)
        neighbor_keys = pool[0].reshape(listed * block_rows, HEAD_FEATURES)
        neighbor_values = pool[1].reshape(listed * block_rows, HEAD_FEATURES)
        query_now = group_cols(query_rows, group, group_features).reshape(
            tok_local, group_width, HEAD_FEATURES
        )
        input_now = group_cols(layer_input, group, group_features)
        gain_now = lax.dynamic_slice_in_dim(gain_row, group * group_features, group_features, 0)
        grad_now = head_grad.reshape(tok_local, group_width, HEAD_FEATURES)
        scores = (
            jnp.einsum("bhd,jd->hbj", query_now, neighbor_keys, preferred_element_type=jnp.float32)
            * scale_factor
        )
        row_max = jnp.max(scores, axis=-1, keepdims=True)
        weights = jnp.exp(scores - row_max)
        probs = weights / jnp.sum(weights, axis=-1, keepdims=True)
        probs_low = probs.astype(jnp.bfloat16)
        prob_grad = jnp.einsum(
            "bhd,jd->hbj", grad_now, neighbor_values, preferred_element_type=jnp.float32
        )
        row_dot = jnp.sum(probs * prob_grad, axis=-1, keepdims=True)
        score_grad = (probs * (prob_grad - row_dot)).astype(jnp.bfloat16)
        query_grad = (
            jnp.einsum("hbj,jd->bhd", score_grad, neighbor_keys, preferred_element_type=jnp.float32)
            * scale_factor
        ).reshape(tok_local, group_features)
        key_part = (
            jnp.einsum("hbj,bhd->jd", score_grad, query_now, preferred_element_type=jnp.float32)
            * scale_factor
        )
        value_part = jnp.einsum(
            "hbj,bhd->jd", probs_low, grad_now, preferred_element_type=jnp.float32
        )
        moved_grad = (gain_now * query_grad).astype(jnp.bfloat16)
        handed = (head_grad.astype(jnp.float32) + moved_grad.astype(jnp.float32)).astype(
            jnp.bfloat16
        )
        gain_part = jnp.sum(input_now.astype(jnp.float32) * query_grad, axis=0)
        parts = jnp.stack([key_part, value_part]).reshape(2, listed, block_rows, HEAD_FEATURES)
        return handed, parts, gain_part

    incoming = jnp.zeros((tok_local, group_features), jnp.bfloat16)
    handed_turns, part_turns, gain_turns = [], [], []
    for turn in range(turn_count):
        group = jnp.clip(turn - lag, 0, kv_heads - 1)
        from_top = group_cols(own_top, group, group_features)
        head_grad = jnp.where(on_top, from_top, incoming)
        handed, parts, gain_part = attend(group, head_grad)
        handed_turns.append(handed)
        part_turns.append(parts)
        gain_turns.append(gain_part)
        if turn + 1 < turn_count:
            incoming = passed_along(handed, "section", -1)

    def own_turns(pieces):
        stacked = jnp.stack(pieces)
        return lax.dynamic_slice_in_dim(stacked, lag, kv_heads, 0)

    stream_out = own_turns(handed_turns).transpose(1, 0, 2).reshape(tok_local, feature_count)
    all_parts = own_turns(part_turns).transpose(1, 2, 3, 0, 4).reshape(
        2, listed, block_rows, kv_width
    )
    from_next = cyclic_shift(all_parts[:, 0], "ctx", -1)
    from_prev = cyclic_shift(all_parts[:, 2], "ctx", 1)
    extra_part = all_parts[:, 3]
    lanes_back = jnp.where(
        lane_users[:, None, None, None], extra_part[None], jnp.zeros_like(extra_part)[None]
    )
    gain_full = own_turns(gain_turns).reshape(feature_count)
    summed = lax.psum(jnp.concatenate([lanes_back.reshape(-1), gain_full]), "ctx")
    lanes_sum = summed[: lanes_back.size].reshape(lanes_back.shape)
    extra_back = jnp.sum(
        jnp.where(lane_sources[:, None, None, None], lanes_sum, jnp.zeros_like(lanes_sum)), axis=0
    )
    kv_total = all_parts[:, 1] + from_next + from_prev + extra_back
    kv_out = kv_total.astype(jnp.bfloat16)
    gain_ctx = lax.dynamic_slice_in_dim(summed[lanes_back.size :], ctx_pos * gain_width, gain_width, 0)
    gain_total = lax.psum(gain_ctx, "dp")
    return (stream_out[None, None], kv_out[0][None, None], kv_out[1][None, None], gain_total[None])


def solution(mesh):
    placed = (
        P("section", "dp", "ctx", None),
        P("section", "dp", "ctx", None),
        P("section", "dp", "ctx", None),
        P("section", "ctx"),
        P("dp", "ctx", None),
        P(),
    )
    return jax.shard_map(
        shards,
        mesh=mesh,
        in_specs=placed,
        out_specs=(
            P("section", "dp", "ctx", None),
            P("section", "dp", "ctx", None),
            P("section", "dp", "ctx", None),
            P("section", "ctx"),
        ),
        check_vma=False,
    )
```

```python
import math

import jax
import jax.numpy as jnp
from jax import lax
from jax.sharding import PartitionSpec as P

HEAD_FEATURES = 128


def passed_along(block, axis, distance):
    devices = range(lax.axis_size(axis))
    route = [(i - distance, i) for i in devices if i - distance in devices]
    return lax.ppermute(block, axis, route)


def cyclic_shift(block, axis, distance):
    count = lax.axis_size(axis)
    return lax.ppermute(block, axis, [(i, (i + distance) % count) for i in range(count)])


def shards(query_input, key_states, value_states, query_gain, top_grad, block_lists):
    ctx_count = lax.axis_size("ctx")
    section_count = lax.axis_size("section")
    section_pos = lax.axis_index("section")
    ctx_pos = lax.axis_index("ctx")
    layer_input = query_input[0, 0]
    tok_local, feature_count = layer_input.shape
    kv_width = key_states.shape[-1]
    kv_heads = kv_width // HEAD_FEATURES
    head_count = feature_count // HEAD_FEATURES
    group_width = head_count // kv_heads
    group_features = group_width * HEAD_FEATURES
    gain_width = query_gain.shape[-1]
    block_count, listed = block_lists.shape
    block_rows = tok_local
    assert block_count == ctx_count and listed == 4
    scale_factor = 1.0 / math.sqrt(HEAD_FEATURES)
    turn_count = kv_heads + section_count - 1
    last = ctx_count - 1

    first_row = block_lists[0]
    first_extra = jnp.sum(
        jnp.where((first_row != last) & (first_row != 0) & (first_row != 1), first_row, 0)
    )
    last_row = block_lists[last]
    last_extra = jnp.sum(
        jnp.where((last_row != last - 1) & (last_row != last) & (last_row != 0), last_row, 0)
    )
    is_first = ctx_pos == 0
    is_last = ctx_pos == last
    is_second = ctx_pos == 1
    uses_zero = ~(is_first | is_last | is_second)
    lane_sources = jnp.stack([ctx_pos == 0, ctx_pos == first_extra, ctx_pos == last_extra, is_last])
    lane_users = jnp.stack([uses_zero, is_first, is_last, is_second])

    gain_own = query_gain[0]
    gain_high = gain_own.astype(jnp.bfloat16)
    gain_rest = gain_own - gain_high.astype(jnp.float32)
    gain_mid = gain_rest.astype(jnp.bfloat16)
    gain_low = (gain_rest - gain_mid.astype(jnp.float32)).astype(jnp.bfloat16)
    gain_placed = lax.dynamic_update_slice_in_dim(
        jnp.zeros((3, feature_count), jnp.bfloat16),
        jnp.stack([gain_high, gain_mid, gain_low]),
        ctx_pos * gain_width,
        1,
    )
    own_kv = jnp.stack([key_states[0, 0], value_states[0, 0]])
    lanes_out = jnp.where(lane_sources[:, None, None, None], own_kv[None], jnp.zeros_like(own_kv)[None])
    came_in = lax.psum(jnp.concatenate([lanes_out.reshape(-1), gain_placed.reshape(-1)]), "ctx")
    lanes_in = came_in[: lanes_out.size].reshape(lanes_out.shape)
    gain_pieces = came_in[lanes_out.size :].reshape(3, feature_count).astype(jnp.float32)
    gain_row = (gain_pieces[0] + gain_pieces[1]) + gain_pieces[2]
    extra_kv = jnp.sum(
        jnp.where(lane_users[:, None, None, None], lanes_in, jnp.zeros_like(lanes_in)), axis=0
    )
    prev_kv = cyclic_shift(own_kv, "ctx", 1)
    next_kv = cyclic_shift(own_kv, "ctx", -1)
    pool_kv = jnp.stack([prev_kv, own_kv, next_kv, extra_kv], axis=1)

    query_rows = (layer_input.astype(jnp.float32) * gain_row).astype(jnp.bfloat16)
    own_top = top_grad[0]
    on_top = section_pos == section_count - 1
    lag = section_count - 1 - section_pos

    def group_cols(array, group, width):
        return lax.dynamic_slice_in_dim(array, group * width, width, array.ndim - 1)

    def attend(group, head_grad):
        pool = group_cols(pool_kv, group, HEAD_FEATURES)
        neighbor_keys = pool[0].reshape(listed * block_rows, HEAD_FEATURES)
        neighbor_values = pool[1].reshape(listed * block_rows, HEAD_FEATURES)
        query_now = group_cols(query_rows, group, group_features).reshape(
            tok_local, group_width, HEAD_FEATURES
        )
        input_now = group_cols(layer_input, group, group_features)
        gain_now = lax.dynamic_slice_in_dim(gain_row, group * group_features, group_features, 0)
        grad_now = head_grad.reshape(tok_local, group_width, HEAD_FEATURES)
        scores = (
            jnp.einsum("bhd,jd->hbj", query_now, neighbor_keys, preferred_element_type=jnp.float32)
            * scale_factor
        )
        row_max = jnp.max(scores, axis=-1, keepdims=True)
        weights = jnp.exp(scores - row_max)
        probs = weights / jnp.sum(weights, axis=-1, keepdims=True)
        probs_low = probs.astype(jnp.bfloat16)
        prob_grad = jnp.einsum(
            "bhd,jd->hbj", grad_now, neighbor_values, preferred_element_type=jnp.float32
        )
        row_dot = jnp.sum(probs * prob_grad, axis=-1, keepdims=True)
        score_grad = (probs * (prob_grad - row_dot)).astype(jnp.bfloat16)
        query_grad = (
            jnp.einsum("hbj,jd->bhd", score_grad, neighbor_keys, preferred_element_type=jnp.float32)
            * scale_factor
        ).reshape(tok_local, group_features)
        key_part = (
            jnp.einsum("hbj,bhd->jd", score_grad, query_now, preferred_element_type=jnp.float32)
            * scale_factor
        )
        value_part = jnp.einsum(
            "hbj,bhd->jd", probs_low, grad_now, preferred_element_type=jnp.float32
        )
        moved_grad = (gain_now * query_grad).astype(jnp.bfloat16)
        handed = (head_grad.astype(jnp.float32) + moved_grad.astype(jnp.float32)).astype(
            jnp.bfloat16
        )
        gain_part = jnp.sum(input_now.astype(jnp.float32) * query_grad, axis=0)
        parts = jnp.stack([key_part, value_part]).reshape(2, listed, block_rows, HEAD_FEATURES)
        return handed, parts, gain_part

    incoming = jnp.zeros((tok_local, group_features), jnp.bfloat16)
    handed_turns, part_turns, gain_turns = [], [], []
    for turn in range(turn_count):
        group = jnp.clip(turn - lag, 0, kv_heads - 1)
        from_top = group_cols(own_top, group, group_features)
        head_grad = jnp.where(on_top, from_top, incoming)
        handed, parts, gain_part = attend(group, head_grad)
        handed_turns.append(handed)
        part_turns.append(parts)
        gain_turns.append(gain_part)
        if turn + 1 < turn_count:
            incoming = passed_along(handed, "section", -1)

    def own_turns(pieces):
        stacked = jnp.stack(pieces)
        return lax.dynamic_slice_in_dim(stacked, lag, kv_heads, 0)

    stream_out = own_turns(handed_turns).transpose(1, 0, 2).reshape(tok_local, feature_count)
    all_parts = own_turns(part_turns).transpose(1, 2, 3, 0, 4).reshape(
        2, listed, block_rows, kv_width
    )
    from_next = cyclic_shift(all_parts[:, 0], "ctx", -1)
    from_prev = cyclic_shift(all_parts[:, 2], "ctx", 1)
    extra_part = all_parts[:, 3]
    lanes_back = jnp.where(
        lane_users[:, None, None, None], extra_part[None], jnp.zeros_like(extra_part)[None]
    )
    gain_full = own_turns(gain_turns).reshape(feature_count)
    zero_size = lanes_back[0].size
    summed = lax.psum(jnp.concatenate([lanes_back[0].reshape(-1), gain_full]), "ctx")
    single_sum = lax.psum(lanes_back[1:].astype(jnp.bfloat16), "ctx").astype(jnp.float32)
    lanes_sum = jnp.concatenate([summed[:zero_size].reshape(lanes_back[:1].shape), single_sum])
    extra_back = jnp.sum(
        jnp.where(lane_sources[:, None, None, None], lanes_sum, jnp.zeros_like(lanes_sum)), axis=0
    )
    kv_total = all_parts[:, 1] + from_next + from_prev + extra_back
    kv_out = kv_total.astype(jnp.bfloat16)
    gain_ctx = lax.dynamic_slice_in_dim(summed[zero_size:], ctx_pos * gain_width, gain_width, 0)
    gain_total = lax.psum(gain_ctx, "dp")
    return (stream_out[None, None], kv_out[0][None, None], kv_out[1][None, None], gain_total[None])


def solution(mesh):
    placed = (
        P("section", "dp", "ctx", None),
        P("section", "dp", "ctx", None),
        P("section", "dp", "ctx", None),
        P("section", "ctx"),
        P("dp", "ctx", None),
        P(),
    )
    return jax.shard_map(
        shards,
        mesh=mesh,
        in_specs=placed,
        out_specs=(
            P("section", "dp", "ctx", None),
            P("section", "dp", "ctx", None),
            P("section", "dp", "ctx", None),
            P("section", "ctx"),
        ),
        check_vma=False,
    )
```

```python
import math

import jax
import jax.numpy as jnp
import numpy as np
from jax import lax
from jax.sharding import PartitionSpec as P

HEAD_FEATURES = 128


def passed_along(block, axis, distance):
    devices = range(lax.axis_size(axis))
    route = [(i - distance, i) for i in devices if i - distance in devices]
    return lax.ppermute(block, axis, route)


def shards(query_input, key_states, value_states, query_gain, top_grad, block_lists):
    ctx_count = lax.axis_size("ctx")
    section_count = lax.axis_size("section")
    section_pos = lax.axis_index("section")
    layer_input = query_input[0, 0]
    tok_local, feature_count = layer_input.shape
    kv_width = key_states.shape[-1]
    kv_heads = kv_width // HEAD_FEATURES
    head_count = feature_count // HEAD_FEATURES
    local_heads = head_count // ctx_count
    group_width = head_count // kv_heads
    local_kv = max(1, local_heads // group_width)
    per_kv = local_heads // local_kv
    repeats = ctx_count * local_kv // kv_heads
    local_width = local_heads * HEAD_FEATURES
    slot_width = local_kv * HEAD_FEATURES
    total_rows = tok_local * ctx_count
    block_count, listed = block_lists.shape
    block_rows = total_rows // block_count
    scale_factor = 1.0 / math.sqrt(HEAD_FEATURES)
    slot_index = np.arange(ctx_count * local_kv)
    slot_heads = slot_index // local_kv * local_heads // group_width + slot_index % local_kv
    sent_keys = (
        key_states[0, 0]
        .reshape(tok_local, kv_heads, HEAD_FEATURES)[:, slot_heads]
        .reshape(tok_local, ctx_count * slot_width)
    )
    sent_values = (
        value_states[0, 0]
        .reshape(tok_local, kv_heads, HEAD_FEATURES)[:, slot_heads]
        .reshape(tok_local, ctx_count * slot_width)
    )
    sent_widths = (local_width, local_width, slot_width, slot_width)
    packed = jnp.concatenate(
        [
            piece.reshape(tok_local, ctx_count, width)
            for piece, width in zip(
                (layer_input, top_grad[0], sent_keys, sent_values), sent_widths
            )
        ],
        axis=2,
    ).reshape(tok_local, ctx_count * sum(sent_widths))
    moved = lax.all_to_all(packed, "ctx", split_axis=1, concat_axis=0, tiled=True)
    edges = np.cumsum((0,) + sent_widths)
    head_input, head_top, head_keys, head_values = lax.optimization_barrier(
        tuple(moved[:, edges[i] : edges[i + 1]] for i in range(len(sent_widths)))
    )
    gain_row = query_gain[0]
    query_rows = (head_input.astype(jnp.float32) * gain_row).astype(jnp.bfloat16)
    blocked_keys = head_keys.reshape(block_count, block_rows, local_kv, HEAD_FEATURES)
    blocked_values = head_values.reshape(block_count, block_rows, local_kv, HEAD_FEATURES)
    per_turn = 4
    unit_count = block_count // per_turn
    turn_rows = per_turn * block_rows
    token_rows = turn_rows // ctx_count
    turn_count = unit_count + section_count - 1
    grid_shape = (per_turn, block_rows, local_kv, per_kv, HEAD_FEATURES)

    def attend(unit, head_grad):
        first_row = unit * turn_rows
        query_now = lax.dynamic_slice_in_dim(query_rows, first_row, turn_rows, 0).reshape(
            grid_shape
        )
        input_now = lax.dynamic_slice_in_dim(head_input, first_row, turn_rows, 0)
        grad_now = head_grad.reshape(grid_shape)
        lists_now = lax.dynamic_slice_in_dim(block_lists, unit * per_turn, per_turn, 0)
        neighbor_keys = blocked_keys[lists_now].reshape(
            per_turn, listed * block_rows, local_kv, HEAD_FEATURES
        )
        neighbor_values = blocked_values[lists_now].reshape(
            per_turn, listed * block_rows, local_kv, HEAD_FEATURES
        )
        scores = (
            jnp.einsum(
                "pbkgd,pjkd->pkgbj", query_now, neighbor_keys, preferred_element_type=jnp.float32
            )
            * scale_factor
        )
        row_max = jnp.max(scores, axis=-1, keepdims=True)
        weights = jnp.exp(scores - row_max)
        probs = weights / jnp.sum(weights, axis=-1, keepdims=True)
        probs_low = probs.astype(jnp.bfloat16)
        prob_grad = jnp.einsum(
            "pbkgd,pjkd->pkgbj", grad_now, neighbor_values, preferred_element_type=jnp.float32
        )
        row_dot = jnp.sum(probs * prob_grad, axis=-1, keepdims=True)
        score_grad = (probs * (prob_grad - row_dot)).astype(jnp.bfloat16)
        query_grad = (
            jnp.einsum(
                "pkgbj,pjkd->pbkgd", score_grad, neighbor_keys, preferred_element_type=jnp.float32
            )
            * scale_factor
        )
        key_part = (
            jnp.einsum(
                "pkgbj,pbkgd->pjkd", score_grad, query_now, preferred_element_type=jnp.float32
            )
            * scale_factor
        )
        value_part = jnp.einsum(
            "pkgbj,pbkgd->pjkd", probs_low, grad_now, preferred_element_type=jnp.float32
        )
        query_grad = query_grad.reshape(turn_rows, local_width)
        gain_part = jnp.sum(input_now.astype(jnp.float32) * query_grad, axis=0)
        return (
            query_grad,
            key_part.reshape(per_turn, listed * block_rows, slot_width),
            value_part.reshape(per_turn, listed * block_rows, slot_width),
            gain_part,
        )

    def spare(unit, head_grad):
        empty_part = jnp.zeros((per_turn, listed * block_rows, slot_width), jnp.float32)
        return (
            jnp.zeros((turn_rows, local_width), jnp.float32),
            empty_part,
            empty_part,
            jnp.zeros((local_width,), jnp.float32),
        )

    on_top = section_pos == section_count - 1

    def turn_step(turn, carry):
        incoming, result_heads, key_slots, value_slots, gain_acc = carry
        unit = turn - (section_count - 1 - section_pos)
        active = (unit >= 0) & (unit < unit_count)
        safe_index = jnp.clip(unit, 0, unit_count - 1)
        target = jnp.where(active, safe_index, unit_count)
        from_top = lax.dynamic_slice_in_dim(head_top, safe_index * turn_rows, turn_rows, 0)
        head_grad = jnp.where(on_top, from_top, incoming)
        query_grad, key_part, value_part, gain_part = lax.cond(
            active, attend, spare, safe_index, head_grad
        )
        moved_grad = (gain_row * query_grad).astype(jnp.bfloat16)
        handed = (head_grad.astype(jnp.float32) + moved_grad.astype(jnp.float32)).astype(
            jnp.bfloat16
        )
        result_heads = lax.dynamic_update_slice_in_dim(result_heads, handed, target * turn_rows, 0)
        key_slots = lax.dynamic_update_slice_in_dim(key_slots, key_part, target * per_turn, 0)
        value_slots = lax.dynamic_update_slice_in_dim(value_slots, value_part, target * per_turn, 0)
        gain_acc = gain_acc + gain_part
        incoming = passed_along(handed, "section", -1)
        return (incoming, result_heads, key_slots, value_slots, gain_acc)

    first_incoming = jnp.zeros((turn_rows, local_width), jnp.bfloat16)
    slot_zeros = jnp.zeros(
        ((unit_count + 1) * per_turn, listed * block_rows, slot_width), jnp.float32
    )
    start_carry = (
        first_incoming,
        jnp.zeros(((unit_count + 1) * turn_rows, local_width), jnp.bfloat16),
        slot_zeros,
        slot_zeros,
        jnp.zeros((local_width,), jnp.float32),
    )
    final_carry = lax.fori_loop(0, turn_count, turn_step, start_carry)
    incoming, result_heads, key_slots, value_slots, gain_acc = final_carry
    result_rows = lax.all_to_all(
        result_heads[:total_rows], "ctx", split_axis=0, concat_axis=1, tiled=True
    )
    target_labels = block_lists.reshape(-1)
    key_pieces = key_slots[:block_count].reshape(block_count * listed, block_rows, slot_width)
    value_pieces = value_slots[:block_count].reshape(block_count * listed, block_rows, slot_width)
    key_acc = (
        jnp.zeros((block_count, block_rows, slot_width), jnp.float32)
        .at[target_labels]
        .add(key_pieces)
    )
    value_acc = (
        jnp.zeros((block_count, block_rows, slot_width), jnp.float32)
        .at[target_labels]
        .add(value_pieces)
    )
    key_back, value_back = (
        lax.all_to_all(
            key_acc.reshape(total_rows, slot_width).astype(jnp.bfloat16),
            "ctx",
            split_axis=0,
            concat_axis=1,
            tiled=True,
        ).astype(jnp.float32),
        lax.all_to_all(
            value_acc.reshape(total_rows, slot_width).astype(jnp.bfloat16),
            "ctx",
            split_axis=0,
            concat_axis=1,
            tiled=True,
        ).astype(jnp.float32),
    )
    key_out = (
        key_back.reshape(tok_local, kv_heads, repeats, HEAD_FEATURES)
        .sum(axis=2)
        .reshape(tok_local, kv_width)
        .astype(jnp.bfloat16)
    )
    value_out = (
        value_back.reshape(tok_local, kv_heads, repeats, HEAD_FEATURES)
        .sum(axis=2)
        .reshape(tok_local, kv_width)
        .astype(jnp.bfloat16)
    )
    gain_total = lax.psum(gain_acc, "dp")
    return (result_rows[None, None], key_out[None, None], value_out[None, None], gain_total[None])


def solution(mesh):
    placed = (
        P("section", "dp", "ctx", None),
        P("section", "dp", "ctx", None),
        P("section", "dp", "ctx", None),
        P("section", "ctx"),
        P("dp", "ctx", None),
        P(),
    )
    return jax.shard_map(
        shards,
        mesh=mesh,
        in_specs=placed,
        out_specs=(
            P("section", "dp", "ctx", None),
            P("section", "dp", "ctx", None),
            P("section", "dp", "ctx", None),
            P("section", "ctx"),
        ),
        check_vma=False,
    )
```

```python
import math

import jax
import jax.numpy as jnp
import numpy as np
from jax import lax
from jax.sharding import PartitionSpec as P

HEAD_FEATURES = 128


def passed_along(block, axis, distance):
    devices = range(lax.axis_size(axis))
    route = [(i - distance, i) for i in devices if i - distance in devices]
    return lax.ppermute(block, axis, route)


def shards(query_input, key_states, value_states, query_gain, top_grad, block_lists):
    ctx_count = lax.axis_size("ctx")
    section_count = lax.axis_size("section")
    section_pos = lax.axis_index("section")
    layer_input = query_input[0, 0]
    tok_local, feature_count = layer_input.shape
    kv_width = key_states.shape[-1]
    kv_heads = kv_width // HEAD_FEATURES
    head_count = feature_count // HEAD_FEATURES
    local_heads = head_count // ctx_count
    group_width = head_count // kv_heads
    local_kv = max(1, local_heads // group_width)
    per_kv = local_heads // local_kv
    repeats = ctx_count * local_kv // kv_heads
    local_width = local_heads * HEAD_FEATURES
    slot_width = local_kv * HEAD_FEATURES
    total_rows = tok_local * ctx_count
    block_count, listed = block_lists.shape
    block_rows = total_rows // block_count
    scale_factor = 1.0 / math.sqrt(HEAD_FEATURES)
    slot_index = np.arange(ctx_count * local_kv)
    slot_heads = slot_index // local_kv * local_heads // group_width + slot_index % local_kv
    sent_keys = (
        key_states[0, 0]
        .reshape(tok_local, kv_heads, HEAD_FEATURES)[:, slot_heads]
        .reshape(tok_local, ctx_count * slot_width)
    )
    sent_values = (
        value_states[0, 0]
        .reshape(tok_local, kv_heads, HEAD_FEATURES)[:, slot_heads]
        .reshape(tok_local, ctx_count * slot_width)
    )
    quarter = tok_local // section_count
    top_width = local_width * quarter // tok_local
    top_rows = lax.dynamic_slice_in_dim(top_grad[0], section_pos * quarter, quarter, 0)
    top_piece = (
        top_rows.reshape(quarter, ctx_count, local_width)
        .transpose(1, 0, 2)
        .reshape(ctx_count, tok_local, top_width)
        .transpose(1, 0, 2)
    )
    sent_widths = (local_width, top_width, slot_width, slot_width)
    packed = jnp.concatenate(
        [layer_input.reshape(tok_local, ctx_count, local_width), top_piece]
        + [
            piece.reshape(tok_local, ctx_count, slot_width)
            for piece in (sent_keys, sent_values)
        ],
        axis=2,
    ).reshape(tok_local, ctx_count * sum(sent_widths))
    moved = lax.all_to_all(packed, "ctx", split_axis=1, concat_axis=0, tiled=True)
    edges = np.cumsum((0,) + sent_widths)
    head_input, top_part, head_keys, head_values = lax.optimization_barrier(
        tuple(moved[:, edges[i] : edges[i + 1]] for i in range(len(sent_widths)))
    )
    top_part = top_part.reshape(ctx_count, quarter, local_width)
    top_quarters = [
        lax.ppermute(top_part, "section", [(q, section_count - 1)])
        for q in range(section_count - 1)
    ]
    head_top = jnp.stack(top_quarters + [top_part], axis=1).reshape(total_rows, local_width)
    gain_row = query_gain[0]
    query_rows = (head_input.astype(jnp.float32) * gain_row).astype(jnp.bfloat16)
    blocked_keys = head_keys.reshape(block_count, block_rows, local_kv, HEAD_FEATURES)
    blocked_values = head_values.reshape(block_count, block_rows, local_kv, HEAD_FEATURES)
    per_turn = 2
    unit_count = block_count // per_turn
    turn_rows = per_turn * block_rows
    token_rows = turn_rows // ctx_count
    turn_count = unit_count + section_count - 1
    grid_shape = (per_turn, block_rows, local_kv, per_kv, HEAD_FEATURES)

    def attend(unit, head_grad):
        first_row = unit * turn_rows
        query_now = lax.dynamic_slice_in_dim(query_rows, first_row, turn_rows, 0).reshape(
            grid_shape
        )
        input_now = lax.dynamic_slice_in_dim(head_input, first_row, turn_rows, 0)
        grad_now = head_grad.reshape(grid_shape)
        lists_now = lax.dynamic_slice_in_dim(block_lists, unit * per_turn, per_turn, 0)
        neighbor_keys = blocked_keys[lists_now].reshape(
            per_turn, listed * block_rows, local_kv, HEAD_FEATURES
        )
        neighbor_values = blocked_values[lists_now].reshape(
            per_turn, listed * block_rows, local_kv, HEAD_FEATURES
        )
        scores = (
            jnp.einsum(
                "pbkgd,pjkd->pkgbj", query_now, neighbor_keys, preferred_element_type=jnp.float32
            )
            * scale_factor
        )
        row_max = jnp.max(scores, axis=-1, keepdims=True)
        weights = jnp.exp(scores - row_max)
        probs = weights / jnp.sum(weights, axis=-1, keepdims=True)
        probs_low = probs.astype(jnp.bfloat16)
        prob_grad = jnp.einsum(
            "pbkgd,pjkd->pkgbj", grad_now, neighbor_values, preferred_element_type=jnp.float32
        )
        row_dot = jnp.sum(probs * prob_grad, axis=-1, keepdims=True)
        score_grad = (probs * (prob_grad - row_dot)).astype(jnp.bfloat16)
        query_grad = (
            jnp.einsum(
                "pkgbj,pjkd->pbkgd", score_grad, neighbor_keys, preferred_element_type=jnp.float32
            )
            * scale_factor
        )
        key_part = (
            jnp.einsum(
                "pkgbj,pbkgd->pjkd", score_grad, query_now, preferred_element_type=jnp.float32
            )
            * scale_factor
        )
        value_part = jnp.einsum(
            "pkgbj,pbkgd->pjkd", probs_low, grad_now, preferred_element_type=jnp.float32
        )
        query_grad = query_grad.reshape(turn_rows, local_width)
        gain_part = jnp.sum(input_now.astype(jnp.float32) * query_grad, axis=0)
        return (
            query_grad,
            key_part.reshape(per_turn, listed * block_rows, slot_width),
            value_part.reshape(per_turn, listed * block_rows, slot_width),
            gain_part,
        )

    def spare(unit, head_grad):
        empty_part = jnp.zeros((per_turn, listed * block_rows, slot_width), jnp.float32)
        return (
            jnp.zeros((turn_rows, local_width), jnp.float32),
            empty_part,
            empty_part,
            jnp.zeros((local_width,), jnp.float32),
        )

    on_top = section_pos == section_count - 1

    def turn_step(turn, carry):
        incoming, result_heads, key_slots, value_slots, gain_acc = carry
        unit = turn - (section_count - 1 - section_pos)
        active = (unit >= 0) & (unit < unit_count)
        safe_index = jnp.clip(unit, 0, unit_count - 1)
        target = jnp.where(active, safe_index, unit_count)
        from_top = lax.dynamic_slice_in_dim(head_top, safe_index * turn_rows, turn_rows, 0)
        head_grad = jnp.where(on_top, from_top, incoming)
        query_grad, key_part, value_part, gain_part = lax.cond(
            active, attend, spare, safe_index, head_grad
        )
        moved_grad = (gain_row * query_grad).astype(jnp.bfloat16)
        handed = (head_grad.astype(jnp.float32) + moved_grad.astype(jnp.float32)).astype(
            jnp.bfloat16
        )
        result_heads = lax.dynamic_update_slice_in_dim(result_heads, handed, target * turn_rows, 0)
        key_slots = lax.dynamic_update_slice_in_dim(key_slots, key_part, target * per_turn, 0)
        value_slots = lax.dynamic_update_slice_in_dim(value_slots, value_part, target * per_turn, 0)
        gain_acc = gain_acc + gain_part
        incoming = passed_along(handed, "section", -1)
        return (incoming, result_heads, key_slots, value_slots, gain_acc)

    first_incoming = jnp.zeros((turn_rows, local_width), jnp.bfloat16)
    slot_zeros = jnp.zeros(
        ((unit_count + 1) * per_turn, listed * block_rows, slot_width), jnp.float32
    )
    start_carry = (
        first_incoming,
        jnp.zeros(((unit_count + 1) * turn_rows, local_width), jnp.bfloat16),
        slot_zeros,
        slot_zeros,
        jnp.zeros((local_width,), jnp.float32),
    )
    final_carry = lax.fori_loop(0, turn_count, turn_step, start_carry)
    incoming, result_heads, key_slots, value_slots, gain_acc = final_carry
    result_rows = lax.all_to_all(
        result_heads[:total_rows], "ctx", split_axis=0, concat_axis=1, tiled=True
    )
    target_labels = block_lists.reshape(-1)
    key_pieces = key_slots[:block_count].reshape(block_count * listed, block_rows, slot_width)
    value_pieces = value_slots[:block_count].reshape(block_count * listed, block_rows, slot_width)
    key_acc = (
        jnp.zeros((block_count, block_rows, slot_width), jnp.float32)
        .at[target_labels]
        .add(key_pieces)
    )
    value_acc = (
        jnp.zeros((block_count, block_rows, slot_width), jnp.float32)
        .at[target_labels]
        .add(value_pieces)
    )
    key_back, value_back = (
        lax.all_to_all(
            key_acc.reshape(total_rows, slot_width).astype(jnp.bfloat16),
            "ctx",
            split_axis=0,
            concat_axis=1,
            tiled=True,
        ).astype(jnp.float32),
        lax.all_to_all(
            value_acc.reshape(total_rows, slot_width).astype(jnp.bfloat16),
            "ctx",
            split_axis=0,
            concat_axis=1,
            tiled=True,
        ).astype(jnp.float32),
    )
    key_out = (
        key_back.reshape(tok_local, kv_heads, repeats, HEAD_FEATURES)
        .sum(axis=2)
        .reshape(tok_local, kv_width)
        .astype(jnp.bfloat16)
    )
    value_out = (
        value_back.reshape(tok_local, kv_heads, repeats, HEAD_FEATURES)
        .sum(axis=2)
        .reshape(tok_local, kv_width)
        .astype(jnp.bfloat16)
    )
    gain_total = lax.psum(gain_acc, "dp")
    return (result_rows[None, None], key_out[None, None], value_out[None, None], gain_total[None])


def solution(mesh):
    placed = (
        P("section", "dp", "ctx", None),
        P("section", "dp", "ctx", None),
        P("section", "dp", "ctx", None),
        P("section", "ctx"),
        P("dp", "ctx", None),
        P(),
    )
    return jax.shard_map(
        shards,
        mesh=mesh,
        in_specs=placed,
        out_specs=(
            P("section", "dp", "ctx", None),
            P("section", "dp", "ctx", None),
            P("section", "dp", "ctx", None),
            P("section", "ctx"),
        ),
        check_vma=False,
    )
```

```python
import math

import jax
import jax.numpy as jnp
import numpy as np
from jax import lax
from jax.sharding import PartitionSpec as P

HEAD_FEATURES = 128


def passed_along(block, axis, distance):
    devices = range(lax.axis_size(axis))
    route = [(i - distance, i) for i in devices if i - distance in devices]
    return lax.ppermute(block, axis, route)


def shards(query_input, key_states, value_states, query_gain, top_grad, block_lists):
    ctx_count = lax.axis_size("ctx")
    section_count = lax.axis_size("section")
    section_pos = lax.axis_index("section")
    layer_input = query_input[0, 0]
    tok_local, feature_count = layer_input.shape
    kv_width = key_states.shape[-1]
    kv_heads = kv_width // HEAD_FEATURES
    head_count = feature_count // HEAD_FEATURES
    local_heads = head_count // ctx_count
    group_width = head_count // kv_heads
    local_kv = max(1, local_heads // group_width)
    per_kv = local_heads // local_kv
    repeats = ctx_count * local_kv // kv_heads
    local_width = local_heads * HEAD_FEATURES
    slot_width = local_kv * HEAD_FEATURES
    total_rows = tok_local * ctx_count
    block_count, listed = block_lists.shape
    block_rows = total_rows // block_count
    scale_factor = 1.0 / math.sqrt(HEAD_FEATURES)
    slot_index = np.arange(ctx_count * local_kv)
    slot_heads = slot_index // local_kv * local_heads // group_width + slot_index % local_kv
    sent_keys = (
        key_states[0, 0]
        .reshape(tok_local, kv_heads, HEAD_FEATURES)[:, slot_heads]
        .reshape(tok_local, ctx_count * slot_width)
    )
    sent_values = (
        value_states[0, 0]
        .reshape(tok_local, kv_heads, HEAD_FEATURES)[:, slot_heads]
        .reshape(tok_local, ctx_count * slot_width)
    )
    quarter = tok_local // section_count
    top_width = local_width * quarter // tok_local
    top_rows = lax.dynamic_slice_in_dim(top_grad[0], section_pos * quarter, quarter, 0)
    top_piece = (
        top_rows.reshape(quarter, ctx_count, local_width)
        .transpose(1, 0, 2)
        .reshape(ctx_count, tok_local, top_width)
        .transpose(1, 0, 2)
    )
    sent_widths = (local_width, top_width, slot_width, slot_width)
    packed = jnp.concatenate(
        [layer_input.reshape(tok_local, ctx_count, local_width), top_piece]
        + [
            piece.reshape(tok_local, ctx_count, slot_width)
            for piece in (sent_keys, sent_values)
        ],
        axis=2,
    ).reshape(tok_local, ctx_count * sum(sent_widths))
    moved = lax.all_to_all(packed, "ctx", split_axis=1, concat_axis=0, tiled=True)
    edges = np.cumsum((0,) + sent_widths)
    head_input, top_part, head_keys, head_values = (
        moved[:, edges[i] : edges[i + 1]] for i in range(len(sent_widths))
    )
    top_part = top_part.reshape(ctx_count, quarter, local_width)
    top_quarters = [
        lax.ppermute(top_part, "section", [(q, section_count - 1)])
        for q in range(section_count - 1)
    ]
    head_top = jnp.stack(top_quarters + [top_part], axis=1).reshape(total_rows, local_width)
    head_input, head_top, head_keys, head_values = lax.optimization_barrier(
        (head_input, head_top, head_keys, head_values)
    )
    gain_row = query_gain[0]
    query_rows = (head_input.astype(jnp.float32) * gain_row).astype(jnp.bfloat16)
    blocked_keys = head_keys.reshape(block_count, block_rows, local_kv, HEAD_FEATURES)
    blocked_values = head_values.reshape(block_count, block_rows, local_kv, HEAD_FEATURES)
    per_turn = 2
    unit_count = block_count // per_turn
    turn_rows = per_turn * block_rows
    token_rows = turn_rows // ctx_count
    turn_count = unit_count + section_count - 1
    grid_shape = (per_turn, block_rows, local_kv, per_kv, HEAD_FEATURES)

    def attend(unit, head_grad):
        first_row = unit * turn_rows
        query_now = lax.dynamic_slice_in_dim(query_rows, first_row, turn_rows, 0).reshape(
            grid_shape
        )
        input_now = lax.dynamic_slice_in_dim(head_input, first_row, turn_rows, 0)
        grad_now = head_grad.reshape(grid_shape)
        lists_now = lax.dynamic_slice_in_dim(block_lists, unit * per_turn, per_turn, 0)
        neighbor_keys = blocked_keys[lists_now].reshape(
            per_turn, listed * block_rows, local_kv, HEAD_FEATURES
        )
        neighbor_values = blocked_values[lists_now].reshape(
            per_turn, listed * block_rows, local_kv, HEAD_FEATURES
        )
        scores = (
            jnp.einsum(
                "pbkgd,pjkd->pkgbj", query_now, neighbor_keys, preferred_element_type=jnp.float32
            )
            * scale_factor
        )
        row_max = jnp.max(scores, axis=-1, keepdims=True)
        weights = jnp.exp(scores - row_max)
        probs = weights / jnp.sum(weights, axis=-1, keepdims=True)
        probs_low = probs.astype(jnp.bfloat16)
        prob_grad = jnp.einsum(
            "pbkgd,pjkd->pkgbj", grad_now, neighbor_values, preferred_element_type=jnp.float32
        )
        row_dot = jnp.sum(probs * prob_grad, axis=-1, keepdims=True)
        score_grad = (probs * (prob_grad - row_dot)).astype(jnp.bfloat16)
        query_grad = (
            jnp.einsum(
                "pkgbj,pjkd->pbkgd", score_grad, neighbor_keys, preferred_element_type=jnp.float32
            )
            * scale_factor
        )
        key_part = (
            jnp.einsum(
                "pkgbj,pbkgd->pjkd", score_grad, query_now, preferred_element_type=jnp.float32
            )
            * scale_factor
        )
        value_part = jnp.einsum(
            "pkgbj,pbkgd->pjkd", probs_low, grad_now, preferred_element_type=jnp.float32
        )
        query_grad = query_grad.reshape(turn_rows, local_width)
        gain_part = jnp.sum(input_now.astype(jnp.float32) * query_grad, axis=0)
        return (
            query_grad,
            key_part.reshape(per_turn, listed * block_rows, slot_width),
            value_part.reshape(per_turn, listed * block_rows, slot_width),
            gain_part,
        )

    def spare(unit, head_grad):
        empty_part = jnp.zeros((per_turn, listed * block_rows, slot_width), jnp.float32)
        return (
            jnp.zeros((turn_rows, local_width), jnp.float32),
            empty_part,
            empty_part,
            jnp.zeros((local_width,), jnp.float32),
        )

    on_top = section_pos == section_count - 1

    def turn_step(turn, carry):
        incoming, result_heads, key_slots, value_slots, gain_acc = carry
        unit = turn - (section_count - 1 - section_pos)
        active = (unit >= 0) & (unit < unit_count)
        safe_index = jnp.clip(unit, 0, unit_count - 1)
        target = jnp.where(active, safe_index, unit_count)
        from_top = lax.dynamic_slice_in_dim(head_top, safe_index * turn_rows, turn_rows, 0)
        head_grad = jnp.where(on_top, from_top, incoming)
        query_grad, key_part, value_part, gain_part = lax.cond(
            active, attend, spare, safe_index, head_grad
        )
        moved_grad = (gain_row * query_grad).astype(jnp.bfloat16)
        handed = (head_grad.astype(jnp.float32) + moved_grad.astype(jnp.float32)).astype(
            jnp.bfloat16
        )
        result_heads = lax.dynamic_update_slice_in_dim(result_heads, handed, target * turn_rows, 0)
        key_slots = lax.dynamic_update_slice_in_dim(key_slots, key_part, target * per_turn, 0)
        value_slots = lax.dynamic_update_slice_in_dim(value_slots, value_part, target * per_turn, 0)
        gain_acc = gain_acc + gain_part
        incoming = passed_along(handed, "section", -1)
        return (incoming, result_heads, key_slots, value_slots, gain_acc)

    first_incoming = jnp.zeros((turn_rows, local_width), jnp.bfloat16)
    slot_zeros = jnp.zeros(
        ((unit_count + 1) * per_turn, listed * block_rows, slot_width), jnp.float32
    )
    start_carry = (
        first_incoming,
        jnp.zeros(((unit_count + 1) * turn_rows, local_width), jnp.bfloat16),
        slot_zeros,
        slot_zeros,
        jnp.zeros((local_width,), jnp.float32),
    )
    final_carry = lax.fori_loop(0, turn_count, turn_step, start_carry)
    incoming, result_heads, key_slots, value_slots, gain_acc = final_carry
    result_rows = lax.all_to_all(
        result_heads[:total_rows], "ctx", split_axis=0, concat_axis=1, tiled=True
    )
    target_labels = block_lists.reshape(-1)
    key_pieces = key_slots[:block_count].reshape(block_count * listed, block_rows, slot_width)
    value_pieces = value_slots[:block_count].reshape(block_count * listed, block_rows, slot_width)
    key_acc = (
        jnp.zeros((block_count, block_rows, slot_width), jnp.float32)
        .at[target_labels]
        .add(key_pieces)
    )
    value_acc = (
        jnp.zeros((block_count, block_rows, slot_width), jnp.float32)
        .at[target_labels]
        .add(value_pieces)
    )
    key_back, value_back = (
        lax.all_to_all(
            key_acc.reshape(total_rows, slot_width).astype(jnp.bfloat16),
            "ctx",
            split_axis=0,
            concat_axis=1,
            tiled=True,
        ).astype(jnp.float32),
        lax.all_to_all(
            value_acc.reshape(total_rows, slot_width).astype(jnp.bfloat16),
            "ctx",
            split_axis=0,
            concat_axis=1,
            tiled=True,
        ).astype(jnp.float32),
    )
    key_out = (
        key_back.reshape(tok_local, kv_heads, repeats, HEAD_FEATURES)
        .sum(axis=2)
        .reshape(tok_local, kv_width)
        .astype(jnp.bfloat16)
    )
    value_out = (
        value_back.reshape(tok_local, kv_heads, repeats, HEAD_FEATURES)
        .sum(axis=2)
        .reshape(tok_local, kv_width)
        .astype(jnp.bfloat16)
    )
    gain_total = lax.psum(gain_acc, "dp")
    return (result_rows[None, None], key_out[None, None], value_out[None, None], gain_total[None])


def solution(mesh):
    placed = (
        P("section", "dp", "ctx", None),
        P("section", "dp", "ctx", None),
        P("section", "dp", "ctx", None),
        P("section", "ctx"),
        P("dp", "ctx", None),
        P(),
    )
    return jax.shard_map(
        shards,
        mesh=mesh,
        in_specs=placed,
        out_specs=(
            P("section", "dp", "ctx", None),
            P("section", "dp", "ctx", None),
            P("section", "dp", "ctx", None),
            P("section", "ctx"),
        ),
        check_vma=False,
    )
```

```python
import math

import jax
import jax.numpy as jnp
import numpy as np
from jax import lax
from jax.sharding import PartitionSpec as P

HEAD_FEATURES = 128


def passed_along(block, axis, distance):
    devices = range(lax.axis_size(axis))
    route = [(i - distance, i) for i in devices if i - distance in devices]
    return lax.ppermute(block, axis, route)


def shards(query_input, key_states, value_states, query_gain, top_grad, block_lists):
    ctx_count = lax.axis_size("ctx")
    section_count = lax.axis_size("section")
    section_pos = lax.axis_index("section")
    layer_input = query_input[0, 0]
    tok_local, feature_count = layer_input.shape
    kv_width = key_states.shape[-1]
    kv_heads = kv_width // HEAD_FEATURES
    head_count = feature_count // HEAD_FEATURES
    local_heads = head_count // ctx_count
    group_width = head_count // kv_heads
    local_kv = max(1, local_heads // group_width)
    per_kv = local_heads // local_kv
    repeats = ctx_count * local_kv // kv_heads
    local_width = local_heads * HEAD_FEATURES
    slot_width = local_kv * HEAD_FEATURES
    total_rows = tok_local * ctx_count
    block_count, listed = block_lists.shape
    block_rows = total_rows // block_count
    scale_factor = 1.0 / math.sqrt(HEAD_FEATURES)
    slot_index = np.arange(ctx_count * local_kv)
    slot_heads = slot_index // local_kv * local_heads // group_width + slot_index % local_kv
    sent_keys = (
        key_states[0, 0]
        .reshape(tok_local, kv_heads, HEAD_FEATURES)[:, slot_heads]
        .reshape(tok_local, ctx_count * slot_width)
    )
    sent_values = (
        value_states[0, 0]
        .reshape(tok_local, kv_heads, HEAD_FEATURES)[:, slot_heads]
        .reshape(tok_local, ctx_count * slot_width)
    )
    quarter = tok_local // section_count
    top_width = local_width * quarter // tok_local
    top_rows = lax.dynamic_slice_in_dim(top_grad[0], section_pos * quarter, quarter, 0)
    top_piece = (
        top_rows.reshape(quarter, ctx_count, local_width)
        .transpose(1, 0, 2)
        .reshape(ctx_count, tok_local, top_width)
        .transpose(1, 0, 2)
    )
    sent_widths = (local_width, slot_width, slot_width, top_width)
    packed = jnp.concatenate(
        [layer_input.reshape(tok_local, ctx_count, local_width)]
        + [
            piece.reshape(tok_local, ctx_count, slot_width)
            for piece in (sent_keys, sent_values)
        ]
        + [top_piece],
        axis=2,
    ).reshape(tok_local, ctx_count * sum(sent_widths))
    moved = lax.all_to_all(packed, "ctx", split_axis=1, concat_axis=0, tiled=True)
    edges = np.cumsum((0,) + sent_widths)
    head_input, head_keys, head_values, top_part = (
        moved[:, edges[i] : edges[i + 1]] for i in range(len(sent_widths))
    )
    top_part = top_part.reshape(ctx_count, quarter, local_width)
    top_quarters = [
        lax.ppermute(top_part, "section", [(q, section_count - 1)])
        for q in range(section_count - 1)
    ]
    head_top = jnp.stack(top_quarters + [top_part], axis=1).reshape(total_rows, local_width)
    head_input, head_top, head_keys, head_values = lax.optimization_barrier(
        (head_input, head_top, head_keys, head_values)
    )
    gain_row = query_gain[0]
    query_rows = (head_input.astype(jnp.float32) * gain_row).astype(jnp.bfloat16)
    blocked_keys = head_keys.reshape(block_count, block_rows, local_kv, HEAD_FEATURES)
    blocked_values = head_values.reshape(block_count, block_rows, local_kv, HEAD_FEATURES)
    per_turn = 2
    unit_count = block_count // per_turn
    turn_rows = per_turn * block_rows
    token_rows = turn_rows // ctx_count
    turn_count = unit_count + section_count - 1
    grid_shape = (per_turn, block_rows, local_kv, per_kv, HEAD_FEATURES)

    def attend(unit, head_grad):
        first_row = unit * turn_rows
        query_now = lax.dynamic_slice_in_dim(query_rows, first_row, turn_rows, 0).reshape(
            grid_shape
        )
        input_now = lax.dynamic_slice_in_dim(head_input, first_row, turn_rows, 0)
        grad_now = head_grad.reshape(grid_shape)
        lists_now = lax.dynamic_slice_in_dim(block_lists, unit * per_turn, per_turn, 0)
        neighbor_keys = blocked_keys[lists_now].reshape(
            per_turn, listed * block_rows, local_kv, HEAD_FEATURES
        )
        neighbor_values = blocked_values[lists_now].reshape(
            per_turn, listed * block_rows, local_kv, HEAD_FEATURES
        )
        scores = (
            jnp.einsum(
                "pbkgd,pjkd->pkgbj", query_now, neighbor_keys, preferred_element_type=jnp.float32
            )
            * scale_factor
        )
        row_max = jnp.max(scores, axis=-1, keepdims=True)
        weights = jnp.exp(scores - row_max)
        probs = weights / jnp.sum(weights, axis=-1, keepdims=True)
        probs_low = probs.astype(jnp.bfloat16)
        prob_grad = jnp.einsum(
            "pbkgd,pjkd->pkgbj", grad_now, neighbor_values, preferred_element_type=jnp.float32
        )
        row_dot = jnp.sum(probs * prob_grad, axis=-1, keepdims=True)
        score_grad = (probs * (prob_grad - row_dot)).astype(jnp.bfloat16)
        query_grad = (
            jnp.einsum(
                "pkgbj,pjkd->pbkgd", score_grad, neighbor_keys, preferred_element_type=jnp.float32
            )
            * scale_factor
        )
        key_part = (
            jnp.einsum(
                "pkgbj,pbkgd->pjkd", score_grad, query_now, preferred_element_type=jnp.float32
            )
            * scale_factor
        )
        value_part = jnp.einsum(
            "pkgbj,pbkgd->pjkd", probs_low, grad_now, preferred_element_type=jnp.float32
        )
        query_grad = query_grad.reshape(turn_rows, local_width)
        gain_part = jnp.sum(input_now.astype(jnp.float32) * query_grad, axis=0)
        return (
            query_grad,
            key_part.reshape(per_turn, listed * block_rows, slot_width),
            value_part.reshape(per_turn, listed * block_rows, slot_width),
            gain_part,
        )

    def spare(unit, head_grad):
        empty_part = jnp.zeros((per_turn, listed * block_rows, slot_width), jnp.float32)
        return (
            jnp.zeros((turn_rows, local_width), jnp.float32),
            empty_part,
            empty_part,
            jnp.zeros((local_width,), jnp.float32),
        )

    on_top = section_pos == section_count - 1

    def turn_step(turn, carry):
        incoming, result_heads, key_slots, value_slots, gain_acc = carry
        unit = turn - (section_count - 1 - section_pos)
        active = (unit >= 0) & (unit < unit_count)
        safe_index = jnp.clip(unit, 0, unit_count - 1)
        target = jnp.where(active, safe_index, unit_count)
        from_top = lax.dynamic_slice_in_dim(head_top, safe_index * turn_rows, turn_rows, 0)
        head_grad = jnp.where(on_top, from_top, incoming)
        query_grad, key_part, value_part, gain_part = lax.cond(
            active, attend, spare, safe_index, head_grad
        )
        moved_grad = (gain_row * query_grad).astype(jnp.bfloat16)
        handed = (head_grad.astype(jnp.float32) + moved_grad.astype(jnp.float32)).astype(
            jnp.bfloat16
        )
        result_heads = lax.dynamic_update_slice_in_dim(result_heads, handed, target * turn_rows, 0)
        key_slots = lax.dynamic_update_slice_in_dim(key_slots, key_part, target * per_turn, 0)
        value_slots = lax.dynamic_update_slice_in_dim(value_slots, value_part, target * per_turn, 0)
        gain_acc = gain_acc + gain_part
        incoming = passed_along(handed, "section", -1)
        return (incoming, result_heads, key_slots, value_slots, gain_acc)

    first_incoming = jnp.zeros((turn_rows, local_width), jnp.bfloat16)
    slot_zeros = jnp.zeros(
        ((unit_count + 1) * per_turn, listed * block_rows, slot_width), jnp.float32
    )
    start_carry = (
        first_incoming,
        jnp.zeros(((unit_count + 1) * turn_rows, local_width), jnp.bfloat16),
        slot_zeros,
        slot_zeros,
        jnp.zeros((local_width,), jnp.float32),
    )
    final_carry = lax.fori_loop(0, turn_count, turn_step, start_carry)
    incoming, result_heads, key_slots, value_slots, gain_acc = final_carry
    result_rows = lax.all_to_all(
        result_heads[:total_rows], "ctx", split_axis=0, concat_axis=1, tiled=True
    )
    target_labels = block_lists.reshape(-1)
    key_pieces = key_slots[:block_count].reshape(block_count * listed, block_rows, slot_width)
    value_pieces = value_slots[:block_count].reshape(block_count * listed, block_rows, slot_width)
    key_acc = (
        jnp.zeros((block_count, block_rows, slot_width), jnp.float32)
        .at[target_labels]
        .add(key_pieces)
    )
    value_acc = (
        jnp.zeros((block_count, block_rows, slot_width), jnp.float32)
        .at[target_labels]
        .add(value_pieces)
    )
    key_back, value_back = (
        lax.all_to_all(
            key_acc.reshape(total_rows, slot_width).astype(jnp.bfloat16),
            "ctx",
            split_axis=0,
            concat_axis=1,
            tiled=True,
        ).astype(jnp.float32),
        lax.all_to_all(
            value_acc.reshape(total_rows, slot_width).astype(jnp.bfloat16),
            "ctx",
            split_axis=0,
            concat_axis=1,
            tiled=True,
        ).astype(jnp.float32),
    )
    key_out = (
        key_back.reshape(tok_local, kv_heads, repeats, HEAD_FEATURES)
        .sum(axis=2)
        .reshape(tok_local, kv_width)
        .astype(jnp.bfloat16)
    )
    value_out = (
        value_back.reshape(tok_local, kv_heads, repeats, HEAD_FEATURES)
        .sum(axis=2)
        .reshape(tok_local, kv_width)
        .astype(jnp.bfloat16)
    )
    gain_total = lax.psum(gain_acc, "dp")
    return (result_rows[None, None], key_out[None, None], value_out[None, None], gain_total[None])


def solution(mesh):
    placed = (
        P("section", "dp", "ctx", None),
        P("section", "dp", "ctx", None),
        P("section", "dp", "ctx", None),
        P("section", "ctx"),
        P("dp", "ctx", None),
        P(),
    )
    return jax.shard_map(
        shards,
        mesh=mesh,
        in_specs=placed,
        out_specs=(
            P("section", "dp", "ctx", None),
            P("section", "dp", "ctx", None),
            P("section", "dp", "ctx", None),
            P("section", "ctx"),
        ),
        check_vma=False,
    )
```

```python
import math

import jax
import jax.numpy as jnp
import numpy as np
from jax import lax
from jax.sharding import PartitionSpec as P

HEAD_FEATURES = 128


def passed_along(block, axis, distance):
    devices = range(lax.axis_size(axis))
    route = [(i - distance, i) for i in devices if i - distance in devices]
    return lax.ppermute(block, axis, route)


def shards(query_input, key_states, value_states, query_gain, top_grad, block_lists):
    ctx_count = lax.axis_size("ctx")
    section_count = lax.axis_size("section")
    section_pos = lax.axis_index("section")
    layer_input = query_input[0, 0]
    tok_local, feature_count = layer_input.shape
    kv_width = key_states.shape[-1]
    kv_heads = kv_width // HEAD_FEATURES
    head_count = feature_count // HEAD_FEATURES
    local_heads = head_count // ctx_count
    group_width = head_count // kv_heads
    local_kv = max(1, local_heads // group_width)
    per_kv = local_heads // local_kv
    repeats = ctx_count * local_kv // kv_heads
    local_width = local_heads * HEAD_FEATURES
    slot_width = local_kv * HEAD_FEATURES
    total_rows = tok_local * ctx_count
    block_count, listed = block_lists.shape
    block_rows = total_rows // block_count
    scale_factor = 1.0 / math.sqrt(HEAD_FEATURES)
    slot_index = np.arange(ctx_count * local_kv)
    slot_heads = slot_index // local_kv * local_heads // group_width + slot_index % local_kv
    sent_keys = (
        key_states[0, 0]
        .reshape(tok_local, kv_heads, HEAD_FEATURES)[:, slot_heads]
        .reshape(tok_local, ctx_count * slot_width)
    )
    sent_values = (
        value_states[0, 0]
        .reshape(tok_local, kv_heads, HEAD_FEATURES)[:, slot_heads]
        .reshape(tok_local, ctx_count * slot_width)
    )
    sent_widths = (local_width, local_width, slot_width, slot_width)
    packed = jnp.concatenate(
        [
            piece.reshape(tok_local, ctx_count, width)
            for piece, width in zip(
                (layer_input, top_grad[0], sent_keys, sent_values), sent_widths
            )
        ],
        axis=2,
    ).reshape(tok_local, ctx_count * sum(sent_widths))
    moved = lax.all_to_all(packed, "ctx", split_axis=1, concat_axis=0, tiled=True)
    edges = np.cumsum((0,) + sent_widths)
    head_input, head_top, head_keys, head_values = lax.optimization_barrier(
        tuple(moved[:, edges[i] : edges[i + 1]] for i in range(len(sent_widths)))
    )
    gain_row = query_gain[0]
    query_rows = (head_input.astype(jnp.float32) * gain_row).astype(jnp.bfloat16)
    blocked_keys = head_keys.reshape(block_count, block_rows, local_kv, HEAD_FEATURES)
    blocked_values = head_values.reshape(block_count, block_rows, local_kv, HEAD_FEATURES)
    per_turn = 2
    unit_count = block_count // per_turn
    turn_rows = per_turn * block_rows
    token_rows = turn_rows // ctx_count
    turn_count = unit_count + section_count - 1
    grid_shape = (per_turn, block_rows, local_kv, per_kv, HEAD_FEATURES)

    def attend(unit, head_grad):
        first_row = unit * turn_rows
        query_now = lax.dynamic_slice_in_dim(query_rows, first_row, turn_rows, 0).reshape(
            grid_shape
        )
        input_now = lax.dynamic_slice_in_dim(head_input, first_row, turn_rows, 0)
        grad_now = head_grad.reshape(grid_shape)
        lists_now = lax.dynamic_slice_in_dim(block_lists, unit * per_turn, per_turn, 0)
        neighbor_keys = blocked_keys[lists_now].reshape(
            per_turn, listed * block_rows, local_kv, HEAD_FEATURES
        )
        neighbor_values = blocked_values[lists_now].reshape(
            per_turn, listed * block_rows, local_kv, HEAD_FEATURES
        )
        scores = (
            jnp.einsum(
                "pbkgd,pjkd->pkgbj", query_now, neighbor_keys, preferred_element_type=jnp.float32
            )
            * scale_factor
        )
        row_max = jnp.max(scores, axis=-1, keepdims=True)
        weights = jnp.exp(scores - row_max)
        probs = weights / jnp.sum(weights, axis=-1, keepdims=True)
        probs_low = probs.astype(jnp.bfloat16)
        prob_grad = jnp.einsum(
            "pbkgd,pjkd->pkgbj", grad_now, neighbor_values, preferred_element_type=jnp.float32
        )
        row_dot = jnp.sum(probs * prob_grad, axis=-1, keepdims=True)
        score_grad = (probs * (prob_grad - row_dot)).astype(jnp.bfloat16)
        query_grad = (
            jnp.einsum(
                "pkgbj,pjkd->pbkgd", score_grad, neighbor_keys, preferred_element_type=jnp.float32
            )
            * scale_factor
        )
        key_part = (
            jnp.einsum(
                "pkgbj,pbkgd->pjkd", score_grad, query_now, preferred_element_type=jnp.float32
            )
            * scale_factor
        )
        value_part = jnp.einsum(
            "pkgbj,pbkgd->pjkd", probs_low, grad_now, preferred_element_type=jnp.float32
        )
        query_grad = query_grad.reshape(turn_rows, local_width)
        gain_part = jnp.sum(input_now.astype(jnp.float32) * query_grad, axis=0)
        return (
            query_grad,
            key_part.reshape(per_turn, listed * block_rows, slot_width),
            value_part.reshape(per_turn, listed * block_rows, slot_width),
            gain_part,
        )

    def spare(unit, head_grad):
        empty_part = jnp.zeros((per_turn, listed * block_rows, slot_width), jnp.float32)
        return (
            jnp.zeros((turn_rows, local_width), jnp.float32),
            empty_part,
            empty_part,
            jnp.zeros((local_width,), jnp.float32),
        )

    on_top = section_pos == section_count - 1

    def turn_step(turn, carry):
        incoming, result_heads, key_slots, value_slots, gain_acc = carry
        unit = turn - (section_count - 1 - section_pos)
        active = (unit >= 0) & (unit < unit_count)
        safe_index = jnp.clip(unit, 0, unit_count - 1)
        target = jnp.where(active, safe_index, unit_count)
        from_top = lax.dynamic_slice_in_dim(head_top, safe_index * turn_rows, turn_rows, 0)
        head_grad = jnp.where(on_top, from_top, incoming)
        query_grad, key_part, value_part, gain_part = lax.cond(
            active, attend, spare, safe_index, head_grad
        )
        moved_grad = (gain_row * query_grad).astype(jnp.bfloat16)
        handed = (head_grad.astype(jnp.float32) + moved_grad.astype(jnp.float32)).astype(
            jnp.bfloat16
        )
        result_heads = lax.dynamic_update_slice_in_dim(result_heads, handed, target * turn_rows, 0)
        key_slots = lax.dynamic_update_slice_in_dim(key_slots, key_part, target * per_turn, 0)
        value_slots = lax.dynamic_update_slice_in_dim(value_slots, value_part, target * per_turn, 0)
        gain_acc = gain_acc + gain_part
        incoming = passed_along(handed, "section", -1)
        return (incoming, result_heads, key_slots, value_slots, gain_acc)

    first_incoming = jnp.zeros((turn_rows, local_width), jnp.bfloat16)
    slot_count = (unit_count + 1) * per_turn
    slot_zeros = jnp.zeros((slot_count, listed * block_rows, slot_width), jnp.float32)
    start_carry = (
        first_incoming,
        jnp.zeros(((unit_count + 1) * turn_rows, local_width), jnp.bfloat16),
        slot_zeros,
        slot_zeros,
        jnp.zeros((local_width,), jnp.float32),
    )
    final_carry = lax.fori_loop(0, turn_count, turn_step, start_carry)
    incoming, result_heads, key_slots, value_slots, gain_acc = final_carry
    result_rows = lax.all_to_all(
        result_heads[:total_rows], "ctx", split_axis=0, concat_axis=1, tiled=True
    )
    spare_labels = jnp.full(((slot_count - block_count) * listed,), -1, block_lists.dtype)
    target_labels = jnp.concatenate([block_lists.reshape(-1), spare_labels])
    pick = (target_labels[None, :] == jnp.arange(block_count)[:, None]).astype(jnp.float32)

    def gathered(slots):
        pieces = slots.reshape(slot_count * listed, block_rows, slot_width)
        return jnp.einsum("jb,brc->jrc", pick, pieces, precision=lax.Precision.HIGHEST)

    key_acc = gathered(key_slots)
    value_acc = gathered(value_slots)
    key_back, value_back = (
        lax.all_to_all(
            key_acc.reshape(total_rows, slot_width).astype(jnp.bfloat16),
            "ctx",
            split_axis=0,
            concat_axis=1,
            tiled=True,
        ).astype(jnp.float32),
        lax.all_to_all(
            value_acc.reshape(total_rows, slot_width).astype(jnp.bfloat16),
            "ctx",
            split_axis=0,
            concat_axis=1,
            tiled=True,
        ).astype(jnp.float32),
    )
    key_out = (
        key_back.reshape(tok_local, kv_heads, repeats, HEAD_FEATURES)
        .sum(axis=2)
        .reshape(tok_local, kv_width)
        .astype(jnp.bfloat16)
    )
    value_out = (
        value_back.reshape(tok_local, kv_heads, repeats, HEAD_FEATURES)
        .sum(axis=2)
        .reshape(tok_local, kv_width)
        .astype(jnp.bfloat16)
    )
    gain_total = lax.psum(gain_acc, "dp")
    return (result_rows[None, None], key_out[None, None], value_out[None, None], gain_total[None])


def solution(mesh):
    placed = (
        P("section", "dp", "ctx", None),
        P("section", "dp", "ctx", None),
        P("section", "dp", "ctx", None),
        P("section", "ctx"),
        P("dp", "ctx", None),
        P(),
    )
    return jax.shard_map(
        shards,
        mesh=mesh,
        in_specs=placed,
        out_specs=(
            P("section", "dp", "ctx", None),
            P("section", "dp", "ctx", None),
            P("section", "dp", "ctx", None),
            P("section", "ctx"),
        ),
        check_vma=False,
    )
```

```python
import math

import jax
import jax.numpy as jnp
import numpy as np
from jax import lax
from jax.sharding import PartitionSpec as P

HEAD_FEATURES = 128


def passed_along(block, axis, distance):
    devices = range(lax.axis_size(axis))
    route = [(i - distance, i) for i in devices if i - distance in devices]
    return lax.ppermute(block, axis, route)


def shards(query_input, key_states, value_states, query_gain, top_grad, block_lists):
    ctx_count = lax.axis_size("ctx")
    section_count = lax.axis_size("section")
    section_pos = lax.axis_index("section")
    layer_input = query_input[0, 0]
    tok_local, feature_count = layer_input.shape
    kv_width = key_states.shape[-1]
    kv_heads = kv_width // HEAD_FEATURES
    head_count = feature_count // HEAD_FEATURES
    local_heads = head_count // ctx_count
    group_width = head_count // kv_heads
    local_kv = max(1, local_heads // group_width)
    per_kv = local_heads // local_kv
    repeats = ctx_count * local_kv // kv_heads
    local_width = local_heads * HEAD_FEATURES
    slot_width = local_kv * HEAD_FEATURES
    total_rows = tok_local * ctx_count
    block_count, listed = block_lists.shape
    block_rows = total_rows // block_count
    scale_factor = 1.0 / math.sqrt(HEAD_FEATURES)
    slot_index = np.arange(ctx_count * local_kv)
    slot_heads = slot_index // local_kv * local_heads // group_width + slot_index % local_kv
    sent_keys = (
        key_states[0, 0]
        .reshape(tok_local, kv_heads, HEAD_FEATURES)[:, slot_heads]
        .reshape(tok_local, ctx_count * slot_width)
    )
    sent_values = (
        value_states[0, 0]
        .reshape(tok_local, kv_heads, HEAD_FEATURES)[:, slot_heads]
        .reshape(tok_local, ctx_count * slot_width)
    )
    sent_widths = (local_width, local_width, slot_width, slot_width)
    packed = jnp.concatenate(
        [
            piece.reshape(tok_local, ctx_count, width)
            for piece, width in zip(
                (layer_input, top_grad[0], sent_keys, sent_values), sent_widths
            )
        ],
        axis=2,
    ).reshape(tok_local, ctx_count * sum(sent_widths))
    moved = lax.all_to_all(packed, "ctx", split_axis=1, concat_axis=0, tiled=True)
    edges = np.cumsum((0,) + sent_widths)
    head_input, head_top, head_keys, head_values = lax.optimization_barrier(
        tuple(moved[:, edges[i] : edges[i + 1]] for i in range(len(sent_widths)))
    )
    gain_row = query_gain[0]
    query_rows = (head_input.astype(jnp.float32) * gain_row).astype(jnp.bfloat16)
    blocked_keys = head_keys.reshape(block_count, block_rows, local_kv, HEAD_FEATURES)
    blocked_values = head_values.reshape(block_count, block_rows, local_kv, HEAD_FEATURES)
    per_turn = 2
    unit_count = block_count // per_turn
    turn_rows = per_turn * block_rows
    token_rows = turn_rows // ctx_count
    turn_count = unit_count + section_count - 1
    grid_shape = (per_turn, block_rows, local_kv, per_kv, HEAD_FEATURES)

    def attend(unit, head_grad):
        first_row = unit * turn_rows
        query_now = lax.dynamic_slice_in_dim(query_rows, first_row, turn_rows, 0).reshape(
            grid_shape
        )
        input_now = lax.dynamic_slice_in_dim(head_input, first_row, turn_rows, 0)
        grad_now = head_grad.reshape(grid_shape)
        lists_now = lax.dynamic_slice_in_dim(block_lists, unit * per_turn, per_turn, 0)
        neighbor_keys = blocked_keys[lists_now].reshape(
            per_turn, listed * block_rows, local_kv, HEAD_FEATURES
        )
        neighbor_values = blocked_values[lists_now].reshape(
            per_turn, listed * block_rows, local_kv, HEAD_FEATURES
        )
        scores = (
            jnp.einsum(
                "pbkgd,pjkd->pkgbj", query_now, neighbor_keys, preferred_element_type=jnp.float32
            )
            * scale_factor
        )
        row_max = jnp.max(scores, axis=-1, keepdims=True)
        weights = jnp.exp(scores - row_max)
        probs = weights / jnp.sum(weights, axis=-1, keepdims=True)
        probs_low = probs.astype(jnp.bfloat16)
        prob_grad = jnp.einsum(
            "pbkgd,pjkd->pkgbj", grad_now, neighbor_values, preferred_element_type=jnp.float32
        )
        row_dot = jnp.sum(probs * prob_grad, axis=-1, keepdims=True)
        score_grad = (probs * (prob_grad - row_dot)).astype(jnp.bfloat16)
        query_grad = (
            jnp.einsum(
                "pkgbj,pjkd->pbkgd", score_grad, neighbor_keys, preferred_element_type=jnp.float32
            )
            * scale_factor
        )
        key_part = (
            jnp.einsum(
                "pkgbj,pbkgd->pjkd", score_grad, query_now, preferred_element_type=jnp.float32
            )
            * scale_factor
        )
        value_part = jnp.einsum(
            "pkgbj,pbkgd->pjkd", probs_low, grad_now, preferred_element_type=jnp.float32
        )
        query_grad = query_grad.reshape(turn_rows, local_width)
        gain_part = jnp.sum(input_now.astype(jnp.float32) * query_grad, axis=0)
        return (
            query_grad,
            key_part.reshape(per_turn, listed * block_rows, slot_width),
            value_part.reshape(per_turn, listed * block_rows, slot_width),
            gain_part,
        )

    def spare(unit, head_grad):
        empty_part = jnp.zeros((per_turn, listed * block_rows, slot_width), jnp.float32)
        return (
            jnp.zeros((turn_rows, local_width), jnp.float32),
            empty_part,
            empty_part,
            jnp.zeros((local_width,), jnp.float32),
        )

    on_top = section_pos == section_count - 1

    def turn_step(turn, carry):
        incoming, result_heads, key_slots, value_slots, gain_acc = carry
        unit = turn - (section_count - 1 - section_pos)
        active = (unit >= 0) & (unit < unit_count)
        safe_index = jnp.clip(unit, 0, unit_count - 1)
        target = jnp.where(active, safe_index, unit_count)
        from_top = lax.dynamic_slice_in_dim(head_top, safe_index * turn_rows, turn_rows, 0)
        head_grad = jnp.where(on_top, from_top, incoming)
        query_grad, key_part, value_part, gain_part = lax.cond(
            active, attend, spare, safe_index, head_grad
        )
        moved_grad = (gain_row * query_grad).astype(jnp.bfloat16)
        handed = (head_grad.astype(jnp.float32) + moved_grad.astype(jnp.float32)).astype(
            jnp.bfloat16
        )
        result_heads = lax.dynamic_update_slice_in_dim(result_heads, handed, target * turn_rows, 0)
        key_slots = lax.dynamic_update_slice_in_dim(key_slots, key_part, target * per_turn, 0)
        value_slots = lax.dynamic_update_slice_in_dim(value_slots, value_part, target * per_turn, 0)
        gain_acc = gain_acc + gain_part
        incoming = passed_along(handed, "section", -1)
        return (incoming, result_heads, key_slots, value_slots, gain_acc)

    first_incoming = jnp.zeros((turn_rows, local_width), jnp.bfloat16)
    slot_count = (unit_count + 1) * per_turn
    slot_zeros = jnp.zeros((slot_count, listed * block_rows, slot_width), jnp.float32)
    start_carry = (
        first_incoming,
        jnp.zeros(((unit_count + 1) * turn_rows, local_width), jnp.bfloat16),
        slot_zeros,
        slot_zeros,
        jnp.zeros((local_width,), jnp.float32),
    )
    final_carry = lax.fori_loop(0, turn_count, turn_step, start_carry)
    incoming, result_heads, key_slots, value_slots, gain_acc = final_carry
    result_rows = lax.all_to_all(
        result_heads[:total_rows], "ctx", split_axis=0, concat_axis=1, tiled=True
    )
    spare_labels = jnp.full(((slot_count - block_count) * listed,), -1, block_lists.dtype)
    target_labels = jnp.concatenate([block_lists.reshape(-1), spare_labels])
    pick = (target_labels[None, :] == jnp.arange(block_count)[:, None]).astype(jnp.float32)

    def gathered(slots):
        pieces = slots.reshape(slot_count * listed, block_rows, slot_width)
        return jnp.einsum("jb,brc->jrc", pick, pieces, precision=lax.Precision.HIGHEST)

    key_acc = gathered(key_slots)
    value_acc = gathered(value_slots)
    kv_back = lax.all_to_all(
        jnp.concatenate(
            [
                key_acc.reshape(total_rows, slot_width),
                value_acc.reshape(total_rows, slot_width),
            ],
            axis=1,
        ).astype(jnp.bfloat16),
        "ctx",
        split_axis=0,
        concat_axis=1,
        tiled=True,
    ).astype(jnp.float32).reshape(tok_local, ctx_count, 2, slot_width)
    key_back = kv_back[:, :, 0].reshape(tok_local, ctx_count * slot_width)
    value_back = kv_back[:, :, 1].reshape(tok_local, ctx_count * slot_width)
    key_out = (
        key_back.reshape(tok_local, kv_heads, repeats, HEAD_FEATURES)
        .sum(axis=2)
        .reshape(tok_local, kv_width)
        .astype(jnp.bfloat16)
    )
    value_out = (
        value_back.reshape(tok_local, kv_heads, repeats, HEAD_FEATURES)
        .sum(axis=2)
        .reshape(tok_local, kv_width)
        .astype(jnp.bfloat16)
    )
    gain_total = lax.psum(gain_acc, "dp")
    return (result_rows[None, None], key_out[None, None], value_out[None, None], gain_total[None])


def solution(mesh):
    placed = (
        P("section", "dp", "ctx", None),
        P("section", "dp", "ctx", None),
        P("section", "dp", "ctx", None),
        P("section", "ctx"),
        P("dp", "ctx", None),
        P(),
    )
    return jax.shard_map(
        shards,
        mesh=mesh,
        in_specs=placed,
        out_specs=(
            P("section", "dp", "ctx", None),
            P("section", "dp", "ctx", None),
            P("section", "dp", "ctx", None),
            P("section", "ctx"),
        ),
        check_vma=False,
    )
```
